256 devices in a mesh: dp: 32 (over x, y, core), mp: 8 (over z).
Axes of the slice: x: 4, y: 4, z: 8, core: 2. Of those that a mesh axis runs over, the one named last changes fastest.
Arguments:
- hidden: bfloat16 [512, 1024], P('dp'), may hold values from -6 to 6
- attn_gain: float32 [1024], replicated, may hold values from 0.25 to 1.75
- w_qkv: bfloat16 [1024, 3, 1024], P(None, None, 'mp'), may hold values from -2 to 2
- w_out: bfloat16 [1024, 1024], P('mp'), may hold values from -0.1875 to 0.1875
- mlp_gain: float32 [1024], replicated, may hold values from 0.25 to 1.75
- w_gate_up: bfloat16 [1024, 2, 4096], P(None, None, 'mp'), may hold values from -0.1875 to 0.1875
- w_down: bfloat16 [4096, 1024], P('mp'), may hold values from -0.09375 to 0.09375
- kv_cache: bfloat16 [2, 4096, 128, 1024], P(None, 'dp', None, 'mp'), may hold values from -9 to 9
- lengths: int32 [512], replicated, may hold values from 1 to 16384, as said below
- page_request: int32 [4096], P('dp'), may hold values from -1 to 511, as said below
- page_index: int32 [4096], P('dp'), may hold values from 0 to 127, as said below
Outputs:
- appended: bfloat16 [2, 512, 1024], P(None, 'dp', 'mp')
- hidden_out: bfloat16 [512, 1024], P('dp')
The draws below stay inside these ranges and needn't reach their ends.
Inputs may be any that keep to these rules, and one draw needn't show every extreme that they name: `lengths`: 4 requests hold exactly 16384 tokens, the others fewer than 512. `page_request`: each request owns exactly ceil(lengths / 128) pool pages, which may lie on any data devices; -1 marks an empty page. `page_index`: the pages of a request carry the places 0 to ceil(lengths / 128) - 1, each once; empty pages carry 0.
All inputs are finite; a program needn't handle non-finite values.
Results may differ from the reference program's by a relative error of at most 0.0085.
Values may be sent and summed in bfloat16 or wider, within the bound.
No kernel may reach another device: no remote copies, remote signals or barrier semaphores. Data moves between devices by JAX's collectives and lax.ppermute only.
A program may use at most 128 MiB of HBM per device.

```python
import math
import jax
import jax.numpy as jnp
from jax import lax

D = 1024
FF = 4096
HEADS = 16
HEAD_DIM = 64
PAGE = 128
MAX_PAGES = 128
POOL = 128
REQS = 512
TOTAL_PAGES = 4096
LONG = 4


def paged_plan(key):
    base_key = jax.random.fold_in(key, 7103)
    k_level, k_offset, k_long, k_bias, k_jitter = jax.random.split(base_key, 5)
    top_level = (4 * PAGE).bit_length() - 1
    levels = jax.random.randint(k_level, (REQS,), 0, top_level)
    level_base = jnp.left_shift(jnp.int32(1), levels)
    short_len = level_base + jax.random.randint(k_offset, (REQS,), 0, 1 << 20) % level_base
    chosen = jax.random.permutation(k_long, REQS)[:LONG]
    is_long = jnp.zeros((REQS,), jnp.int32).at[chosen].set(1)
    lengths = jnp.where(is_long > 0, MAX_PAGES * PAGE, short_len).astype(jnp.int32)
    page_counts = (lengths + PAGE - 1) // PAGE
    page_ends = jnp.cumsum(page_counts)
    page_starts = page_ends - page_counts
    used_pages = page_ends[-1]
    devices = TOTAL_PAGES // POOL
    device_bias = jax.random.randint(k_bias, (devices,), 0, 4)
    jitters = jax.random.randint(k_jitter, (TOTAL_PAGES,), 0, 1024)
    slot_ids = jnp.arange(TOTAL_PAGES, dtype=jnp.int32)
    priority = (device_bias[slot_ids // POOL] * 1024 + jitters) * 16384 + slot_ids
    visit = jnp.argsort(priority)
    slot_rank = jnp.argsort(visit).astype(jnp.int32)
    owner_ids = jnp.searchsorted(page_ends, slot_rank, side='right').astype(jnp.int32)
    clamped = jnp.minimum(owner_ids, REQS - 1)
    filled = slot_rank < used_pages
    request_ids = jnp.where(filled, clamped, -1).astype(jnp.int32)
    page_places = jnp.where(filled, slot_rank - page_starts[clamped], 0).astype(jnp.int32)
    return (lengths, request_ids, page_places)


def draw_lengths(key, part):
    return paged_plan(key)[0]


def draw_page_request(key, part):
    return paged_plan(key)[1]


def draw_page_index(key, part):
    return paged_plan(key)[2]


def special_heads(key):
    head_order = jax.random.permutation(jax.random.fold_in(key, 5309), HEADS)
    chosen_count = max(1, HEADS // 4)
    head_flags = jnp.zeros((HEADS,), jnp.float32).at[head_order[:chosen_count]].set(1.0)
    return head_flags


def draw_w_qkv(key, part):
    head_flags = special_heads(key)
    column_flags = jnp.repeat(head_flags, HEAD_DIM)
    query_flags = (jnp.arange(3) == 0).astype(jnp.float32)
    random_key = jax.random.fold_in(key, 811)
    full_shape = (D, 3, HEADS * HEAD_DIM)
    random_part = jnp.clip(jax.random.normal(random_key, full_shape, jnp.float32), -4.0, 4.0)
    strength = 25.0
    offset = strength / math.sqrt(D * HEAD_DIM)
    return (random_part / math.sqrt(D) + offset * query_flags[None, :, None] * column_flags[None, None, :]).astype(jnp.bfloat16)


def draw_kv_cache(key, part):
    head_flags = special_heads(key)
    base_key = jax.random.fold_in(key, 2203)
    pick_key, random_key = jax.random.split(base_key)
    aligned = (jax.random.randint(pick_key, (TOTAL_PAGES, PAGE, HEADS), 0, 16) == 0).astype(jnp.float32) * head_flags
    full_shape = (2, TOTAL_PAGES, PAGE, HEADS, HEAD_DIM)
    random_part = jnp.clip(jax.random.normal(random_key, full_shape, jnp.float32), -4.5, 4.5)
    raised = 4.0
    slot_flags = (jnp.arange(2) == 0).astype(jnp.float32)
    lifted = random_part + raised * slot_flags[:, None, None, None, None] * aligned[None, :, :, :, None]
    return lifted.reshape(2, TOTAL_PAGES, PAGE, HEADS * HEAD_DIM).astype(jnp.bfloat16)


def block_levels(stream_key, dims, cuts, smallest, top_value):
    def one(axis_at, shards_of):
        draws = jax.random.uniform(jax.random.fold_in(jax.random.fold_in(stream_key, 6), axis_at), (shards_of,), jnp.float32, smallest / len(cuts), top_value / len(cuts))
        return jnp.repeat(jnp.exp(draws), dims[axis_at] // shards_of).reshape((-1,) + (1,) * (len(dims) - axis_at - 1))

    factor_of = one(*cuts[0])
    for cut in cuts[1:]:
        factor_of = factor_of * one(*cut)
    return factor_of


def normal_values(rng, dims, deviation, reach, cuts=(), held_as=jnp.bfloat16):
    array = deviation * jax.random.normal(rng, dims, jnp.float32)
    if cuts:
        array = array * block_levels(rng, dims, cuts, -0.22, 0.18)
    return jnp.clip(array, -reach, reach).astype(held_as)


def setup_inputs(seed: int = 0) -> dict:
    key_list = jax.random.split(jax.random.key(seed), 12)
    hidden = normal_values(key_list[0], (REQS, D), 1.0, 6.0, ((0, 32),))
    attn_gain = jnp.clip(1.0 + 0.15 * jax.random.normal(key_list[1], (D,), jnp.float32), 0.25, 1.75)
    w_qkv = draw_w_qkv(jax.random.fold_in(key_list[11], 71), 0)
    w_out = normal_values(key_list[3], (HEADS * HEAD_DIM, D), (HEADS * HEAD_DIM) ** -0.5, 0.1875, ((0, 8),))
    mlp_gain = jnp.clip(1.0 + 0.15 * jax.random.normal(key_list[4], (D,), jnp.float32), 0.25, 1.75)
    w_gate_up = normal_values(key_list[5], (D, 2, FF), D ** -0.5, 0.1875, ((2, 8),))
    w_down = normal_values(key_list[6], (FF, D), FF ** -0.5, 0.09375, ((0, 8),))
    kv_cache = draw_kv_cache(jax.random.fold_in(key_list[11], 71), 0)
    lengths = draw_lengths(jax.random.fold_in(key_list[11], 71), 0)
    page_request = draw_page_request(jax.random.fold_in(key_list[11], 71), 0)
    page_index = draw_page_index(jax.random.fold_in(key_list[11], 71), 0)
    return {"hidden": hidden, "attn_gain": attn_gain, "w_qkv": w_qkv, "w_out": w_out, "mlp_gain": mlp_gain, "w_gate_up": w_gate_up, "w_down": w_down, "kv_cache": kv_cache, "lengths": lengths, "page_request": page_request, "page_index": page_index}


EPSILON = 1e-05
NEGATIVE = -1e+30

def rms_norm(values, gain):
    widened = values.astype(jnp.float32)
    mean_square = lax.optimization_barrier(jnp.mean(widened * widened, axis=-1, keepdims=True))
    return (widened * lax.rsqrt(mean_square + EPSILON) * gain).astype(jnp.bfloat16)

def reference(hidden, attn_gain, w_qkv, w_out, mlp_gain, w_gate_up, w_down, kv_cache, lengths, page_request, page_index):
    head_cols = HEADS * HEAD_DIM
    score_scale = HEAD_DIM ** (-0.5)
    normed = rms_norm(hidden, attn_gain)
    projected = jnp.dot(normed, w_qkv.reshape(D, 3 * head_cols), preferred_element_type=jnp.float32)
    projected = lax.optimization_barrier(projected.astype(jnp.bfloat16)).reshape(REQS, 3, head_cols)
    appended = jnp.stack([projected[:, 1], projected[:, 2]])
    queries = projected[:, 0].reshape(REQS, HEADS, HEAD_DIM).astype(jnp.float32)
    new_keys = projected[:, 1].reshape(REQS, HEADS, HEAD_DIM).astype(jnp.float32)
    new_values = projected[:, 2].reshape(REQS, HEADS, HEAD_DIM).astype(jnp.float32)
    self_scores = lax.optimization_barrier(jnp.sum(queries * new_keys, axis=-1)) * score_scale
    request_ids = jnp.arange(REQS, dtype=jnp.int32)
    offsets = jnp.arange(PAGE, dtype=jnp.int32)

    def block_pages(block_index):
        start = block_index * POOL
        fetched = lax.dynamic_slice_in_dim(kv_cache, start, POOL, 1)
        key_rows = fetched[0].reshape(POOL, PAGE, HEADS, HEAD_DIM).astype(jnp.float32)
        value_rows = fetched[1].reshape(POOL, PAGE, HEADS, HEAD_DIM).astype(jnp.float32)
        owners = lax.dynamic_slice_in_dim(page_request, start, POOL, 0)
        page_pos = lax.dynamic_slice_in_dim(page_index, start, POOL, 0)
        clamped = jnp.maximum(owners, 0)
        scores = jnp.einsum('phd,pthd->pht', queries[clamped], key_rows) * score_scale
        position = page_pos[:, None] * PAGE + offsets[None, :]
        usable = (owners[:, None] >= 0) & (position < lengths[clamped][:, None])
        page_max = lax.optimization_barrier(jnp.max(jnp.where(usable[:, None, :], scores, NEGATIVE), axis=2))
        member = owners[:, None] == request_ids[None, :]
        return (scores, usable, page_max, value_rows, member, clamped, owners)

    def max_step(running_max, block_index):
        scores, usable, page_max, value_rows, member, clamped, owners = block_pages(block_index)
        candidate = lax.optimization_barrier(jnp.max(jnp.where(member[:, :, None], page_max[:, None, :], NEGATIVE), axis=0))
        return (jnp.maximum(running_max, candidate), None)
    blocks = jnp.arange(TOTAL_PAGES // POOL, dtype=jnp.int32)
    running_max, _ = lax.scan(max_step, self_scores, blocks)

    def sum_step(carry, block_index):
        totals, weighted = carry
        scores, usable, page_max, value_rows, member, clamped, owners = block_pages(block_index)
        raw = jnp.where(usable[:, None, :], jnp.exp(scores - page_max[:, :, None]), 0.0)
        page_total = lax.optimization_barrier(jnp.sum(raw, axis=2))
        rounded = lax.optimization_barrier(raw.astype(jnp.bfloat16)).astype(jnp.float32)
        page_sum = jnp.einsum('pht,pthd->phd', rounded, value_rows)
        factors = jnp.where(owners[:, None] >= 0, jnp.exp(page_max - running_max[clamped]), 0.0)
        onehot = member.astype(jnp.float32)
        totals = totals + jnp.einsum('pr,ph->rh', onehot, page_total * factors, precision=lax.Precision.HIGHEST)
        weighted = weighted + jnp.einsum('pr,phd->rhd', onehot, page_sum * factors[:, :, None], precision=lax.Precision.HIGHEST)
        return ((totals, weighted), None)
    self_weight = jnp.exp(self_scores - running_max)
    (totals, weighted), _ = lax.scan(sum_step, (self_weight, self_weight[:, :, None] * new_values), blocks)
    context = (weighted / totals[:, :, None]).reshape(REQS, head_cols).astype(jnp.bfloat16)
    attended = jnp.dot(context, w_out, preferred_element_type=jnp.float32)
    residual = lax.optimization_barrier((hidden.astype(jnp.float32) + attended).astype(jnp.bfloat16))
    normed_mlp = rms_norm(residual, mlp_gain)
    gate_up = jnp.dot(normed_mlp, w_gate_up.reshape(D, 2 * FF), preferred_element_type=jnp.float32).reshape(REQS, 2, FF)
    activated = (jax.nn.silu(gate_up[:, 0]) * gate_up[:, 1]).astype(jnp.bfloat16)
    lowered = jnp.dot(activated, w_down, preferred_element_type=jnp.float32)
    hidden_out = (residual.astype(jnp.float32) + lowered).astype(jnp.bfloat16)
    return (appended, hidden_out)
```

```python
import jax
import jax.numpy as jnp
from jax import lax
from jax.sharding import PartitionSpec as P

HEAD_DIM = 64


EPSILON = 1e-05
NEGATIVE = -1e30


def rms_norm(values, gain):
    widened = values.astype(jnp.float32)
    mean_square = jnp.mean(widened * widened, axis=-1, keepdims=True)
    return (widened * lax.rsqrt(mean_square + EPSILON) * gain).astype(jnp.bfloat16)


def body(
    hidden,
    attn_gain,
    w_qkv,
    w_out,
    mlp_gain,
    w_gate_up,
    w_down,
    kv_cache,
    lengths,
    page_request,
    page_index,
):
    local_rows = hidden.shape[0]
    head_cols = w_qkv.shape[2]
    local_heads = head_cols // HEAD_DIM
    pool_pages = kv_cache.shape[1]
    page_len = kv_cache.shape[2]
    data_devices = lax.axis_size("dp")
    requests = local_rows * data_devices
    score_scale = HEAD_DIM ** (-0.5)
    normed = rms_norm(hidden, attn_gain)
    projected = jnp.dot(
        normed, w_qkv.reshape(w_qkv.shape[0], 3 * head_cols), preferred_element_type=jnp.float32
    )
    projected = lax.optimization_barrier(projected.astype(jnp.bfloat16)).reshape(
        local_rows, 3, head_cols
    )
    appended = jnp.stack([projected[:, 1], projected[:, 2]])
    every_query = lax.all_gather(projected[:, 0], "dp", axis=0, tiled=True)
    own_queries = projected[:, 0].reshape(local_rows, local_heads, HEAD_DIM).astype(jnp.float32)
    own_keys = projected[:, 1].reshape(local_rows, local_heads, HEAD_DIM).astype(jnp.float32)
    own_values = projected[:, 2].reshape(local_rows, local_heads, HEAD_DIM).astype(jnp.float32)
    self_scores = jnp.sum(own_queries * own_keys, axis=-1) * score_scale
    home_row = lax.axis_index("dp") * local_rows
    request_ids = jnp.arange(requests, dtype=jnp.int32)
    offsets = jnp.arange(page_len, dtype=jnp.int32)

    owners = page_request
    clamped = jnp.maximum(owners, 0)
    chosen_queries = every_query[clamped].reshape(pool_pages, local_heads, HEAD_DIM)
    key_rows = kv_cache[0].reshape(pool_pages, page_len, local_heads, HEAD_DIM)
    value_rows = kv_cache[1].reshape(pool_pages, page_len, local_heads, HEAD_DIM)
    scores = (
        jnp.einsum("phd,pthd->pht", chosen_queries, key_rows, preferred_element_type=jnp.float32)
        * score_scale
    )
    position = page_index[:, None] * page_len + offsets[None, :]
    usable = (owners[:, None] >= 0) & (position < lengths[clamped][:, None])
    page_max = jnp.max(jnp.where(usable[:, None, :], scores, NEGATIVE), axis=2)
    raw = jnp.where(usable[:, None, :], jnp.exp(scores - page_max[:, :, None]), 0.0)
    page_total = jnp.sum(raw, axis=2)
    page_sum = jnp.einsum(
        "pht,pthd->phd", raw.astype(jnp.bfloat16), value_rows, preferred_element_type=jnp.float32
    )

    member = owners[:, None] == request_ids[None, :]
    seg_max = jnp.max(jnp.where(member[:, :, None], page_max[:, None, :], NEGATIVE), axis=0)
    self_full = lax.dynamic_update_slice(
        jnp.full((requests, local_heads), NEGATIVE, jnp.float32), self_scores, (home_row, 0)
    )
    local_max = jnp.maximum(seg_max, self_full)
    factors = jnp.where(owners[:, None] >= 0, jnp.exp(page_max - local_max[clamped]), 0.0)
    payload = jnp.concatenate(
        [(page_sum * factors[:, :, None]).reshape(pool_pages, head_cols), page_total * factors],
        axis=1,
    )
    onehot = member.astype(jnp.float32)
    local_sums = jnp.einsum("pr,pc->rc", onehot, payload, precision=lax.Precision.HIGHEST)
    home_max = lax.dynamic_slice_in_dim(local_max, home_row, local_rows, 0)
    self_weight = jnp.exp(self_scores - home_max)
    self_payload = jnp.concatenate(
        [(self_weight[:, :, None] * own_values).reshape(local_rows, head_cols), self_weight],
        axis=1,
    )
    local_sums = local_sums + lax.dynamic_update_slice(
        jnp.zeros_like(local_sums), self_payload, (home_row, 0)
    )

    global_max = lax.pmax(local_max, "dp")
    shrink = jnp.exp(local_max - global_max)
    shrink_cols = jnp.concatenate([jnp.repeat(shrink, HEAD_DIM, axis=1), shrink], axis=1)
    mine = lax.psum_scatter(local_sums * shrink_cols, "dp", scatter_dimension=0, tiled=True)
    own_weighted = mine[:, :head_cols].reshape(local_rows, local_heads, HEAD_DIM)
    own_totals = mine[:, head_cols:]
    context = (
        (own_weighted / own_totals[:, :, None]).reshape(local_rows, head_cols).astype(jnp.bfloat16)
    )
    attended = lax.psum(jnp.dot(context, w_out, preferred_element_type=jnp.float32), "mp")
    residual = lax.optimization_barrier(
        (hidden.astype(jnp.float32) + attended).astype(jnp.bfloat16)
    )
    normed_mlp = rms_norm(residual, mlp_gain)
    hidden_cols = w_gate_up.shape[2]
    gate_up = jnp.dot(
        normed_mlp,
        w_gate_up.reshape(w_gate_up.shape[0], 2 * hidden_cols),
        preferred_element_type=jnp.float32,
    ).reshape(local_rows, 2, hidden_cols)
    activated = (jax.nn.silu(gate_up[:, 0]) * gate_up[:, 1]).astype(jnp.bfloat16)
    lowered = lax.psum(jnp.dot(activated, w_down, preferred_element_type=jnp.float32), "mp")
    hidden_out = (residual.astype(jnp.float32) + lowered).astype(jnp.bfloat16)
    return (appended, hidden_out)


def solution(mesh):
    return jax.shard_map(
        body,
        mesh=mesh,
        in_specs=(
            P("dp", None),
            P(),
            P(None, None, "mp"),
            P("mp", None),
            P(),
            P(None, None, "mp"),
            P("mp", None),
            P(None, "dp", None, "mp"),
            P(),
            P("dp"),
            P("dp"),
        ),
        out_specs=(P(None, "dp", "mp"), P("dp", None)),
        check_vma=False,
    )
```

```python
import jax
import jax.numpy as jnp
from jax import lax
from jax.sharding import PartitionSpec as P

HEAD_DIM = 64


EPSILON = 1e-05
NEGATIVE = -1e30


def rms_norm(values, gain):
    widened = values.astype(jnp.float32)
    mean_square = jnp.mean(widened * widened, axis=-1, keepdims=True)
    return (widened * lax.rsqrt(mean_square + EPSILON) * gain).astype(jnp.bfloat16)


def butterfly_sum(value, axis):
    size = lax.axis_size(axis)
    if size & (size - 1):
        return lax.psum(value, axis)
    distance = 1
    while distance < size:
        pairs = [(j, j ^ distance) for j in range(size)]
        value = value + lax.ppermute(value, axis, pairs)
        distance *= 2
    return value


def butterfly_gather(value, axis):
    size = lax.axis_size(axis)
    if size & (size - 1):
        return lax.all_gather(value, axis, axis=0, tiled=True)
    me = lax.axis_index(axis)
    distance = 1
    while distance < size:
        pairs = [(j, j ^ distance) for j in range(size)]
        other = lax.ppermute(value, axis, pairs)
        low = (me & distance) == 0
        value = jnp.where(
            low, jnp.concatenate([value, other], 0), jnp.concatenate([other, value], 0)
        )
        distance *= 2
    return value


def body(
    hidden,
    attn_gain,
    w_qkv,
    w_out,
    mlp_gain,
    w_gate_up,
    w_down,
    kv_cache,
    lengths,
    page_request,
    page_index,
):
    local_rows = hidden.shape[0]
    head_cols = w_qkv.shape[2]
    local_heads = head_cols // HEAD_DIM
    pool_pages = kv_cache.shape[1]
    page_len = kv_cache.shape[2]
    data_devices = lax.axis_size("dp")
    requests = local_rows * data_devices
    score_scale = HEAD_DIM ** (-0.5)
    normed = rms_norm(hidden, attn_gain)
    projected = jnp.dot(
        normed, w_qkv.reshape(w_qkv.shape[0], 3 * head_cols), preferred_element_type=jnp.float32
    )
    projected = lax.optimization_barrier(projected.astype(jnp.bfloat16)).reshape(
        local_rows, 3, head_cols
    )
    appended = jnp.stack([projected[:, 1], projected[:, 2]])
    every_query = butterfly_gather(projected[:, 0], "dp")
    own_queries = projected[:, 0].reshape(local_rows, local_heads, HEAD_DIM).astype(jnp.float32)
    own_keys = projected[:, 1].reshape(local_rows, local_heads, HEAD_DIM).astype(jnp.float32)
    own_values = projected[:, 2].reshape(local_rows, local_heads, HEAD_DIM).astype(jnp.float32)
    self_scores = jnp.sum(own_queries * own_keys, axis=-1) * score_scale
    home_row = lax.axis_index("dp") * local_rows
    request_ids = jnp.arange(requests, dtype=jnp.int32)
    offsets = jnp.arange(page_len, dtype=jnp.int32)

    owners = page_request
    clamped = jnp.maximum(owners, 0)
    chosen_queries = every_query[clamped].reshape(pool_pages, local_heads, HEAD_DIM)
    key_rows = kv_cache[0].reshape(pool_pages, page_len, local_heads, HEAD_DIM)
    value_rows = kv_cache[1].reshape(pool_pages, page_len, local_heads, HEAD_DIM)
    scores = (
        jnp.einsum("phd,pthd->pht", chosen_queries, key_rows, preferred_element_type=jnp.float32)
        * score_scale
    )
    position = page_index[:, None] * page_len + offsets[None, :]
    usable = (owners[:, None] >= 0) & (position < lengths[clamped][:, None])
    page_max = jnp.max(jnp.where(usable[:, None, :], scores, NEGATIVE), axis=2)
    raw = jnp.where(usable[:, None, :], jnp.exp(scores - page_max[:, :, None]), 0.0)
    page_total = jnp.sum(raw, axis=2)
    page_sum = jnp.einsum(
        "pht,pthd->phd", raw.astype(jnp.bfloat16), value_rows, preferred_element_type=jnp.float32
    )

    member = owners[:, None] == request_ids[None, :]
    seg_max = jnp.max(jnp.where(member[:, :, None], page_max[:, None, :], NEGATIVE), axis=0)
    self_full = lax.dynamic_update_slice(
        jnp.full((requests, local_heads), NEGATIVE, jnp.float32), self_scores, (home_row, 0)
    )
    local_max = jnp.maximum(seg_max, self_full)
    factors = jnp.where(owners[:, None] >= 0, jnp.exp(page_max - local_max[clamped]), 0.0)
    payload = jnp.concatenate(
        [(page_sum * factors[:, :, None]).reshape(pool_pages, head_cols), page_total * factors],
        axis=1,
    )
    onehot = member.astype(jnp.float32)
    local_sums = jnp.einsum("pr,pc->rc", onehot, payload, precision=lax.Precision.HIGHEST)
    home_max = lax.dynamic_slice_in_dim(local_max, home_row, local_rows, 0)
    self_weight = jnp.exp(self_scores - home_max)
    self_payload = jnp.concatenate(
        [(self_weight[:, :, None] * own_values).reshape(local_rows, head_cols), self_weight],
        axis=1,
    )
    local_sums = local_sums + lax.dynamic_update_slice(
        jnp.zeros_like(local_sums), self_payload, (home_row, 0)
    )

    packed = jnp.concatenate([local_sums, local_max], axis=1)
    packed = packed.reshape(data_devices, local_rows, packed.shape[1])
    received = lax.all_to_all(packed, "dp", 0, 0, tiled=True)
    source_max = received[:, :, head_cols + local_heads :]
    global_max = jnp.max(source_max, axis=0)
    shrink = jnp.exp(source_max - global_max[None])
    shrink_cols = jnp.concatenate([jnp.repeat(shrink, HEAD_DIM, axis=2), shrink], axis=2)
    mine = jnp.sum(received[:, :, : head_cols + local_heads] * shrink_cols, axis=0)
    own_weighted = mine[:, :head_cols].reshape(local_rows, local_heads, HEAD_DIM)
    own_totals = mine[:, head_cols:]
    context = (
        (own_weighted / own_totals[:, :, None]).reshape(local_rows, head_cols).astype(jnp.bfloat16)
    )
    attended = butterfly_sum(jnp.dot(context, w_out, preferred_element_type=jnp.float32), "mp")
    residual = lax.optimization_barrier(
        (hidden.astype(jnp.float32) + attended).astype(jnp.bfloat16)
    )
    normed_mlp = rms_norm(residual, mlp_gain)
    hidden_cols = w_gate_up.shape[2]
    gate_up = jnp.dot(
        normed_mlp,
        w_gate_up.reshape(w_gate_up.shape[0], 2 * hidden_cols),
        preferred_element_type=jnp.float32,
    ).reshape(local_rows, 2, hidden_cols)
    activated = (jax.nn.silu(gate_up[:, 0]) * gate_up[:, 1]).astype(jnp.bfloat16)
    lowered = butterfly_sum(jnp.dot(activated, w_down, preferred_element_type=jnp.float32), "mp")
    hidden_out = (residual.astype(jnp.float32) + lowered).astype(jnp.bfloat16)
    return (appended, hidden_out)


def solution(mesh):
    return jax.shard_map(
        body,
        mesh=mesh,
        in_specs=(
            P("dp", None),
            P(),
            P(None, None, "mp"),
            P("mp", None),
            P(),
            P(None, None, "mp"),
            P("mp", None),
            P(None, "dp", None, "mp"),
            P(),
            P("dp"),
            P("dp"),
        ),
        out_specs=(P(None, "dp", "mp"), P("dp", None)),
        check_vma=False,
    )
```

```python
import jax
import jax.numpy as jnp
from jax import lax
from jax.sharding import PartitionSpec as P

HEAD_DIM = 64


EPSILON = 1e-05
NEGATIVE = -1e30


def rms_norm(values, gain):
    widened = values.astype(jnp.float32)
    mean_square = jnp.mean(widened * widened, axis=-1, keepdims=True)
    return (widened * lax.rsqrt(mean_square + EPSILON) * gain).astype(jnp.bfloat16)


def butterfly_sum(value, axis):
    size = lax.axis_size(axis)
    if size & (size - 1):
        return lax.psum(value, axis)
    distance = 1
    while distance < size:
        pairs = [(j, j ^ distance) for j in range(size)]
        value = value + lax.ppermute(value, axis, pairs)
        distance *= 2
    return value


def exchange_gather(value, axis):
    size = lax.axis_size(axis)
    spread = jnp.broadcast_to(value[None], (size,) + value.shape)
    gathered = lax.all_to_all(spread, axis, 0, 0, tiled=True)
    return gathered.reshape((size * value.shape[0],) + value.shape[1:])


def butterfly_gather(value, axis):
    size = lax.axis_size(axis)
    if size & (size - 1):
        return lax.all_gather(value, axis, axis=0, tiled=True)
    me = lax.axis_index(axis)
    distance = 1
    while distance < size:
        pairs = [(j, j ^ distance) for j in range(size)]
        other = lax.ppermute(value, axis, pairs)
        low = (me & distance) == 0
        value = jnp.where(
            low, jnp.concatenate([value, other], 0), jnp.concatenate([other, value], 0)
        )
        distance *= 2
    return value


def body(
    hidden,
    attn_gain,
    w_qkv,
    w_out,
    mlp_gain,
    w_gate_up,
    w_down,
    kv_cache,
    lengths,
    page_request,
    page_index,
):
    local_rows = hidden.shape[0]
    head_cols = w_qkv.shape[2]
    local_heads = head_cols // HEAD_DIM
    pool_pages = kv_cache.shape[1]
    page_len = kv_cache.shape[2]
    data_devices = lax.axis_size("dp")
    requests = local_rows * data_devices
    score_scale = HEAD_DIM ** (-0.5)
    normed = rms_norm(hidden, attn_gain)
    projected = jnp.dot(
        normed, w_qkv.reshape(w_qkv.shape[0], 3 * head_cols), preferred_element_type=jnp.float32
    )
    projected = lax.optimization_barrier(projected.astype(jnp.bfloat16)).reshape(
        local_rows, 3, head_cols
    )
    appended = jnp.stack([projected[:, 1], projected[:, 2]])
    every_query = exchange_gather(projected[:, 0], "dp")
    own_queries = projected[:, 0].reshape(local_rows, local_heads, HEAD_DIM).astype(jnp.float32)
    own_keys = projected[:, 1].reshape(local_rows, local_heads, HEAD_DIM).astype(jnp.float32)
    own_values = projected[:, 2].reshape(local_rows, local_heads, HEAD_DIM).astype(jnp.float32)
    self_scores = jnp.sum(own_queries * own_keys, axis=-1) * score_scale
    home_row = lax.axis_index("dp") * local_rows
    request_ids = jnp.arange(requests, dtype=jnp.int32)
    offsets = jnp.arange(page_len, dtype=jnp.int32)

    owners = page_request
    clamped = jnp.maximum(owners, 0)
    chosen_queries = every_query[clamped]
    head_of_col = jnp.arange(head_cols, dtype=jnp.int32) // HEAD_DIM
    head_mask = head_of_col[:, None] == jnp.arange(local_heads, dtype=jnp.int32)[None, :]
    query_blocks = jnp.where(head_mask[None], chosen_queries[:, :, None], jnp.zeros((), jnp.bfloat16))
    key_rows = kv_cache[0]
    value_rows = kv_cache[1]
    scores = (
        jnp.einsum("ptc,pch->pth", key_rows, query_blocks, preferred_element_type=jnp.float32)
        * score_scale
    )
    position = page_index[:, None] * page_len + offsets[None, :]
    usable = (owners[:, None] >= 0) & (position < lengths[clamped][:, None])
    page_max = jnp.max(jnp.where(usable[:, :, None], scores, NEGATIVE), axis=1)
    raw = jnp.where(usable[:, :, None], jnp.exp(scores - page_max[:, None, :]), 0.0)
    page_total = jnp.sum(raw, axis=1)
    head_sums = jnp.einsum(
        "pth,ptc->phc", raw.astype(jnp.bfloat16), value_rows, preferred_element_type=jnp.float32
    )
    page_sum = jnp.sum(jnp.where(head_mask.T[None], head_sums, 0.0), axis=1)

    member = owners[:, None] == request_ids[None, :]
    seg_max = jnp.max(jnp.where(member[:, :, None], page_max[:, None, :], NEGATIVE), axis=0)
    self_full = lax.dynamic_update_slice(
        jnp.full((requests, local_heads), NEGATIVE, jnp.float32), self_scores, (home_row, 0)
    )
    local_max = jnp.maximum(seg_max, self_full)
    factors = jnp.where(owners[:, None] >= 0, jnp.exp(page_max - local_max[clamped]), 0.0)
    payload = jnp.concatenate(
        [page_sum * jnp.repeat(factors, HEAD_DIM, axis=1), page_total * factors],
        axis=1,
    )
    onehot = member.astype(jnp.float32)
    local_sums = jnp.einsum("pr,pc->rc", onehot, payload, precision=lax.Precision.HIGHEST)
    home_max = lax.dynamic_slice_in_dim(local_max, home_row, local_rows, 0)
    self_weight = jnp.exp(self_scores - home_max)
    self_payload = jnp.concatenate(
        [(self_weight[:, :, None] * own_values).reshape(local_rows, head_cols), self_weight],
        axis=1,
    )
    local_sums = local_sums + lax.dynamic_update_slice(
        jnp.zeros_like(local_sums), self_payload, (home_row, 0)
    )

    packed = jnp.concatenate([local_sums, local_max], axis=1)
    packed = packed.reshape(data_devices, local_rows, packed.shape[1])
    received = lax.all_to_all(packed, "dp", 0, 0, tiled=True)
    source_max = received[:, :, head_cols + local_heads :]
    global_max = jnp.max(source_max, axis=0)
    shrink = jnp.exp(source_max - global_max[None])
    shrink_cols = jnp.concatenate([jnp.repeat(shrink, HEAD_DIM, axis=2), shrink], axis=2)
    mine = jnp.sum(received[:, :, : head_cols + local_heads] * shrink_cols, axis=0)
    own_weighted = mine[:, :head_cols].reshape(local_rows, local_heads, HEAD_DIM)
    own_totals = mine[:, head_cols:]
    context = (
        (own_weighted / own_totals[:, :, None]).reshape(local_rows, head_cols).astype(jnp.bfloat16)
    )
    attended = butterfly_sum(jnp.dot(context, w_out, preferred_element_type=jnp.float32), "mp")
    residual = lax.optimization_barrier(
        (hidden.astype(jnp.float32) + attended).astype(jnp.bfloat16)
    )
    normed_mlp = rms_norm(residual, mlp_gain)
    hidden_cols = w_gate_up.shape[2]
    gate_up = jnp.dot(
        normed_mlp,
        w_gate_up.reshape(w_gate_up.shape[0], 2 * hidden_cols),
        preferred_element_type=jnp.float32,
    ).reshape(local_rows, 2, hidden_cols)
    activated = (jax.nn.silu(gate_up[:, 0]) * gate_up[:, 1]).astype(jnp.bfloat16)
    lowered = butterfly_sum(jnp.dot(activated, w_down, preferred_element_type=jnp.float32), "mp")
    hidden_out = (residual.astype(jnp.float32) + lowered).astype(jnp.bfloat16)
    return (appended, hidden_out)


def solution(mesh):
    return jax.shard_map(
        body,
        mesh=mesh,
        in_specs=(
            P("dp", None),
            P(),
            P(None, None, "mp"),
            P("mp", None),
            P(),
            P(None, None, "mp"),
            P("mp", None),
            P(None, "dp", None, "mp"),
            P(),
            P("dp"),
            P("dp"),
        ),
        out_specs=(P(None, "dp", "mp"), P("dp", None)),
        check_vma=False,
    )
```

```python
import jax
import jax.numpy as jnp
from jax import lax
from jax.sharding import PartitionSpec as P

HEAD_DIM = 64


EPSILON = 1e-05
NEGATIVE = -1e30


def rms_norm(values, gain):
    widened = values.astype(jnp.float32)
    mean_square = jnp.mean(widened * widened, axis=-1, keepdims=True)
    return (widened * lax.rsqrt(mean_square + EPSILON) * gain).astype(jnp.bfloat16)


def butterfly_sum(value, axis):
    size = lax.axis_size(axis)
    if size & (size - 1):
        return lax.psum(value, axis)
    distance = 1
    while distance < size:
        pairs = [(j, j ^ distance) for j in range(size)]
        value = value + lax.ppermute(value, axis, pairs)
        distance *= 2
    return value


def exchange_gather(value, axis):
    size = lax.axis_size(axis)
    spread = jnp.broadcast_to(value[None], (size,) + value.shape)
    gathered = lax.all_to_all(spread, axis, 0, 0, tiled=True)
    return gathered.reshape((size * value.shape[0],) + value.shape[1:])


def butterfly_gather(value, axis):
    size = lax.axis_size(axis)
    if size & (size - 1):
        return lax.all_gather(value, axis, axis=0, tiled=True)
    me = lax.axis_index(axis)
    distance = 1
    while distance < size:
        pairs = [(j, j ^ distance) for j in range(size)]
        other = lax.ppermute(value, axis, pairs)
        low = (me & distance) == 0
        value = jnp.where(
            low, jnp.concatenate([value, other], 0), jnp.concatenate([other, value], 0)
        )
        distance *= 2
    return value


def body(
    hidden,
    attn_gain,
    w_qkv,
    w_out,
    mlp_gain,
    w_gate_up,
    w_down,
    kv_cache,
    lengths,
    page_request,
    page_index,
):
    local_rows = hidden.shape[0]
    head_cols = w_qkv.shape[2]
    local_heads = head_cols // HEAD_DIM
    pool_pages = kv_cache.shape[1]
    page_len = kv_cache.shape[2]
    data_devices = lax.axis_size("dp")
    requests = local_rows * data_devices
    score_scale = HEAD_DIM ** (-0.5)
    normed = rms_norm(hidden, attn_gain)
    projected = jnp.dot(
        normed, w_qkv.reshape(w_qkv.shape[0], 3 * head_cols), preferred_element_type=jnp.float32
    )
    projected = lax.optimization_barrier(projected.astype(jnp.bfloat16)).reshape(
        local_rows, 3, head_cols
    )
    appended = jnp.stack([projected[:, 1], projected[:, 2]])
    every_query = exchange_gather(projected[:, 0], "dp")
    hidden_cols = w_gate_up.shape[2]
    every_query, gate_up_weights = lax.optimization_barrier(
        (every_query, w_gate_up.reshape(w_gate_up.shape[0], 2 * hidden_cols))
    )
    own_queries = projected[:, 0].reshape(local_rows, local_heads, HEAD_DIM).astype(jnp.float32)
    own_keys = projected[:, 1].reshape(local_rows, local_heads, HEAD_DIM).astype(jnp.float32)
    own_values = projected[:, 2].reshape(local_rows, local_heads, HEAD_DIM).astype(jnp.float32)
    self_scores = jnp.sum(own_queries * own_keys, axis=-1) * score_scale
    home_row = lax.axis_index("dp") * local_rows
    request_ids = jnp.arange(requests, dtype=jnp.int32)
    offsets = jnp.arange(page_len, dtype=jnp.int32)

    owners = page_request
    clamped = jnp.maximum(owners, 0)
    chosen_queries = every_query[clamped]
    head_of_col = jnp.arange(head_cols, dtype=jnp.int32) // HEAD_DIM
    head_mask = head_of_col[:, None] == jnp.arange(local_heads, dtype=jnp.int32)[None, :]
    query_blocks = jnp.where(head_mask[None], chosen_queries[:, :, None], jnp.zeros((), jnp.bfloat16))
    key_rows = kv_cache[0]
    value_rows = kv_cache[1]
    scores = (
        jnp.einsum("ptc,pch->pth", key_rows, query_blocks, preferred_element_type=jnp.float32)
        * score_scale
    )
    position = page_index[:, None] * page_len + offsets[None, :]
    usable = (owners[:, None] >= 0) & (position < lengths[clamped][:, None])
    page_max = jnp.max(jnp.where(usable[:, :, None], scores, NEGATIVE), axis=1)
    raw = jnp.where(usable[:, :, None], jnp.exp(scores - page_max[:, None, :]), 0.0)
    page_total = jnp.sum(raw, axis=1)
    head_sums = jnp.einsum(
        "pth,ptc->phc", raw.astype(jnp.bfloat16), value_rows, preferred_element_type=jnp.float32
    )
    page_sum = jnp.sum(jnp.where(head_mask.T[None], head_sums, 0.0), axis=1)

    member = owners[:, None] == request_ids[None, :]
    seg_max = jnp.max(jnp.where(member[:, :, None], page_max[:, None, :], NEGATIVE), axis=0)
    self_full = lax.dynamic_update_slice(
        jnp.full((requests, local_heads), NEGATIVE, jnp.float32), self_scores, (home_row, 0)
    )
    local_max = jnp.maximum(seg_max, self_full)
    factors = jnp.where(owners[:, None] >= 0, jnp.exp(page_max - local_max[clamped]), 0.0)
    payload = jnp.concatenate(
        [page_sum * jnp.repeat(factors, HEAD_DIM, axis=1), page_total * factors],
        axis=1,
    )
    onehot = member.astype(jnp.float32)
    local_sums = jnp.einsum("pr,pc->rc", onehot, payload, precision=lax.Precision.HIGHEST)
    home_max = lax.dynamic_slice_in_dim(local_max, home_row, local_rows, 0)
    self_weight = jnp.exp(self_scores - home_max)
    self_payload = jnp.concatenate(
        [(self_weight[:, :, None] * own_values).reshape(local_rows, head_cols), self_weight],
        axis=1,
    )
    local_sums = local_sums + lax.dynamic_update_slice(
        jnp.zeros_like(local_sums), self_payload, (home_row, 0)
    )

    packed = jnp.concatenate([local_sums, local_max], axis=1)
    packed = packed.reshape(data_devices, local_rows, packed.shape[1])
    received = lax.all_to_all(packed, "dp", 0, 0, tiled=True)
    source_max = received[:, :, head_cols + local_heads :]
    global_max = jnp.max(source_max, axis=0)
    shrink = jnp.exp(source_max - global_max[None])
    shrink_cols = jnp.concatenate([jnp.repeat(shrink, HEAD_DIM, axis=2), shrink], axis=2)
    mine = jnp.sum(received[:, :, : head_cols + local_heads] * shrink_cols, axis=0)
    own_weighted = mine[:, :head_cols].reshape(local_rows, local_heads, HEAD_DIM)
    own_totals = mine[:, head_cols:]
    context = (
        (own_weighted / own_totals[:, :, None]).reshape(local_rows, head_cols).astype(jnp.bfloat16)
    )
    attended = butterfly_sum(jnp.dot(context, w_out, preferred_element_type=jnp.float32), "mp")
    residual = lax.optimization_barrier(
        (hidden.astype(jnp.float32) + attended).astype(jnp.bfloat16)
    )
    normed_mlp = rms_norm(residual, mlp_gain)
    gate_up = jnp.dot(
        normed_mlp,
        gate_up_weights,
        preferred_element_type=jnp.float32,
    ).reshape(local_rows, 2, hidden_cols)
    activated = (jax.nn.silu(gate_up[:, 0]) * gate_up[:, 1]).astype(jnp.bfloat16)
    lowered = butterfly_sum(jnp.dot(activated, w_down, preferred_element_type=jnp.float32), "mp")
    hidden_out = (residual.astype(jnp.float32) + lowered).astype(jnp.bfloat16)
    return (appended, hidden_out)


def solution(mesh):
    return jax.shard_map(
        body,
        mesh=mesh,
        in_specs=(
            P("dp", None),
            P(),
            P(None, None, "mp"),
            P("mp", None),
            P(),
            P(None, None, "mp"),
            P("mp", None),
            P(None, "dp", None, "mp"),
            P(),
            P("dp"),
            P("dp"),
        ),
        out_specs=(P(None, "dp", "mp"), P("dp", None)),
        check_vma=False,
    )
```

```python
import jax
import jax.numpy as jnp
from jax import lax
from jax.sharding import PartitionSpec as P

HEAD_DIM = 64


EPSILON = 1e-05
NEGATIVE = -1e30


def rms_norm(values, gain):
    widened = values.astype(jnp.float32)
    mean_square = jnp.mean(widened * widened, axis=-1, keepdims=True)
    return (widened * lax.rsqrt(mean_square + EPSILON) * gain).astype(jnp.bfloat16)


def butterfly_sum(value, axis):
    size = lax.axis_size(axis)
    if size & (size - 1):
        return lax.psum(value, axis)
    distance = 1
    while distance < size:
        pairs = [(j, j ^ distance) for j in range(size)]
        value = value + lax.ppermute(value, axis, pairs)
        distance *= 2
    return value


def exchange_gather(value, axis):
    size = lax.axis_size(axis)
    spread = jnp.broadcast_to(value[None], (size,) + value.shape)
    gathered = lax.all_to_all(spread, axis, 0, 0, tiled=True)
    return gathered.reshape((size * value.shape[0],) + value.shape[1:])


def butterfly_gather(value, axis):
    size = lax.axis_size(axis)
    if size & (size - 1):
        return lax.all_gather(value, axis, axis=0, tiled=True)
    me = lax.axis_index(axis)
    distance = 1
    while distance < size:
        pairs = [(j, j ^ distance) for j in range(size)]
        other = lax.ppermute(value, axis, pairs)
        low = (me & distance) == 0
        value = jnp.where(
            low, jnp.concatenate([value, other], 0), jnp.concatenate([other, value], 0)
        )
        distance *= 2
    return value


def body(
    hidden,
    attn_gain,
    w_qkv,
    w_out,
    mlp_gain,
    w_gate_up,
    w_down,
    kv_cache,
    lengths,
    page_request,
    page_index,
):
    local_rows = hidden.shape[0]
    head_cols = w_qkv.shape[2]
    local_heads = head_cols // HEAD_DIM
    pool_pages = kv_cache.shape[1]
    page_len = kv_cache.shape[2]
    data_devices = lax.axis_size("dp")
    requests = local_rows * data_devices
    score_scale = HEAD_DIM ** (-0.5)
    normed = rms_norm(hidden, attn_gain)
    projected = jnp.dot(
        normed, w_qkv.reshape(w_qkv.shape[0], 3 * head_cols), preferred_element_type=jnp.float32
    )
    projected = lax.optimization_barrier(projected.astype(jnp.bfloat16)).reshape(
        local_rows, 3, head_cols
    )
    appended = jnp.stack([projected[:, 1], projected[:, 2]])
    every_query = exchange_gather(projected[:, 0], "dp")
    own_queries = projected[:, 0].reshape(local_rows, local_heads, HEAD_DIM).astype(jnp.float32)
    own_keys = projected[:, 1].reshape(local_rows, local_heads, HEAD_DIM).astype(jnp.float32)
    own_values = projected[:, 2].reshape(local_rows, local_heads, HEAD_DIM).astype(jnp.float32)
    self_scores = jnp.sum(own_queries * own_keys, axis=-1) * score_scale
    home_row = lax.axis_index("dp") * local_rows
    request_ids = jnp.arange(requests, dtype=jnp.int32)
    offsets = jnp.arange(page_len, dtype=jnp.int32)

    owners = page_request
    clamped = jnp.maximum(owners, 0)
    chosen_queries = every_query[clamped]
    head_of_col = jnp.arange(head_cols, dtype=jnp.int32) // HEAD_DIM
    head_mask = head_of_col[:, None] == jnp.arange(local_heads, dtype=jnp.int32)[None, :]
    query_blocks = jnp.where(head_mask[None], chosen_queries[:, :, None], jnp.zeros((), jnp.bfloat16))
    key_rows = kv_cache[0]
    value_rows = kv_cache[1]
    scores = (
        jnp.einsum("ptc,pch->pth", key_rows, query_blocks, preferred_element_type=jnp.float32)
        * score_scale
    )
    position = page_index[:, None] * page_len + offsets[None, :]
    usable = (owners[:, None] >= 0) & (position < lengths[clamped][:, None])
    page_max = jnp.max(jnp.where(usable[:, :, None], scores, NEGATIVE), axis=1)
    raw = jnp.where(usable[:, :, None], jnp.exp(scores - page_max[:, None, :]), 0.0)
    page_total = jnp.sum(raw, axis=1)
    head_sums = jnp.einsum(
        "pth,ptc->phc", raw.astype(jnp.bfloat16), value_rows, preferred_element_type=jnp.float32
    )
    page_sum = jnp.sum(jnp.where(head_mask.T[None], head_sums, 0.0), axis=1)

    member = owners[:, None] == request_ids[None, :]
    seg_max = jnp.max(jnp.where(member[:, :, None], page_max[:, None, :], NEGATIVE), axis=0)
    self_full = lax.dynamic_update_slice(
        jnp.full((requests, local_heads), NEGATIVE, jnp.float32), self_scores, (home_row, 0)
    )
    local_max = jnp.maximum(seg_max, self_full)
    factors = jnp.where(owners[:, None] >= 0, jnp.exp(page_max - local_max[clamped]), 0.0)
    payload = jnp.concatenate(
        [page_sum * jnp.repeat(factors, HEAD_DIM, axis=1), page_total * factors],
        axis=1,
    )
    onehot = member.astype(jnp.float32)
    local_sums = jnp.einsum("pr,pc->rc", onehot, payload, precision=lax.Precision.HIGHEST)
    home_max = lax.dynamic_slice_in_dim(local_max, home_row, local_rows, 0)
    self_weight = jnp.exp(self_scores - home_max)
    self_payload = jnp.concatenate(
        [(self_weight[:, :, None] * own_values).reshape(local_rows, head_cols), self_weight],
        axis=1,
    )
    local_sums = local_sums + lax.dynamic_update_slice(
        jnp.zeros_like(local_sums), self_payload, (home_row, 0)
    )

    lanes = 128
    stats = jnp.concatenate([local_sums[:, head_cols:], local_max], axis=1)
    stats = stats.reshape(data_devices, local_rows * 2 * local_heads)
    stats_rows = -(-stats.shape[1] // lanes)
    stats = jnp.pad(stats, ((0, 0), (0, stats_rows * lanes - stats.shape[1])))
    weighted_rows = local_rows * head_cols // lanes
    packed = jnp.concatenate(
        [
            local_sums[:, :head_cols].reshape(data_devices, weighted_rows, lanes),
            stats.reshape(data_devices, stats_rows, lanes),
        ],
        axis=1,
    )
    received = lax.all_to_all(packed, "dp", 0, 0, tiled=True)
    source_weighted = received[:, :weighted_rows].reshape(data_devices, local_rows, head_cols)
    source_stats = received[:, weighted_rows:].reshape(data_devices, stats_rows * lanes)
    source_stats = source_stats[:, : local_rows * 2 * local_heads].reshape(
        data_devices, local_rows, 2 * local_heads
    )
    source_totals = source_stats[:, :, :local_heads]
    source_max = source_stats[:, :, local_heads:]
    global_max = jnp.max(source_max, axis=0)
    shrink = jnp.exp(source_max - global_max[None])
    mine = jnp.concatenate(
        [
            jnp.sum(source_weighted * jnp.repeat(shrink, HEAD_DIM, axis=2), axis=0),
            jnp.sum(source_totals * shrink, axis=0),
        ],
        axis=1,
    )
    own_weighted = mine[:, :head_cols].reshape(local_rows, local_heads, HEAD_DIM)
    own_totals = mine[:, head_cols:]
    context = (
        (own_weighted / own_totals[:, :, None]).reshape(local_rows, head_cols).astype(jnp.bfloat16)
    )
    attended = butterfly_sum(jnp.dot(context, w_out, preferred_element_type=jnp.float32), "mp")
    residual = lax.optimization_barrier(
        (hidden.astype(jnp.float32) + attended).astype(jnp.bfloat16)
    )
    normed_mlp = rms_norm(residual, mlp_gain)
    hidden_cols = w_gate_up.shape[2]
    gate_up = jnp.dot(
        normed_mlp,
        w_gate_up.reshape(w_gate_up.shape[0], 2 * hidden_cols),
        preferred_element_type=jnp.float32,
    ).reshape(local_rows, 2, hidden_cols)
    activated = (jax.nn.silu(gate_up[:, 0]) * gate_up[:, 1]).astype(jnp.bfloat16)
    lowered = butterfly_sum(jnp.dot(activated, w_down, preferred_element_type=jnp.float32), "mp")
    hidden_out = (residual.astype(jnp.float32) + lowered).astype(jnp.bfloat16)
    return (appended, hidden_out)


def solution(mesh):
    return jax.shard_map(
        body,
        mesh=mesh,
        in_specs=(
            P("dp", None),
            P(),
            P(None, None, "mp"),
            P("mp", None),
            P(),
            P(None, None, "mp"),
            P("mp", None),
            P(None, "dp", None, "mp"),
            P(),
            P("dp"),
            P("dp"),
        ),
        out_specs=(P(None, "dp", "mp"), P("dp", None)),
        check_vma=False,
    )
```

```python
import jax
import jax.numpy as jnp
from jax import lax
from jax.sharding import PartitionSpec as P

HEAD_DIM = 64


EPSILON = 1e-05
NEGATIVE = -1e30


def rms_norm(values, gain):
    widened = values.astype(jnp.float32)
    mean_square = jnp.mean(widened * widened, axis=-1, keepdims=True)
    return (widened * lax.rsqrt(mean_square + EPSILON) * gain).astype(jnp.bfloat16)


def butterfly_sum(value, axis):
    size = lax.axis_size(axis)
    if size & (size - 1):
        return lax.psum(value, axis)
    distance = 1
    while distance < size:
        pairs = [(j, j ^ distance) for j in range(size)]
        value = value + lax.ppermute(value, axis, pairs)
        distance *= 2
    return value


def exchange_gather(value, axis):
    size = lax.axis_size(axis)
    spread = jnp.broadcast_to(value[None], (size,) + value.shape)
    gathered = lax.all_to_all(spread, axis, 0, 0, tiled=True)
    return gathered.reshape((size * value.shape[0],) + value.shape[1:])


def butterfly_gather(value, axis):
    size = lax.axis_size(axis)
    if size & (size - 1):
        return lax.all_gather(value, axis, axis=0, tiled=True)
    me = lax.axis_index(axis)
    distance = 1
    while distance < size:
        pairs = [(j, j ^ distance) for j in range(size)]
        other = lax.ppermute(value, axis, pairs)
        low = (me & distance) == 0
        value = jnp.where(
            low, jnp.concatenate([value, other], 0), jnp.concatenate([other, value], 0)
        )
        distance *= 2
    return value


def body(
    hidden,
    attn_gain,
    w_qkv,
    w_out,
    mlp_gain,
    w_gate_up,
    w_down,
    kv_cache,
    lengths,
    page_request,
    page_index,
):
    local_rows = hidden.shape[0]
    head_cols = w_qkv.shape[2]
    local_heads = head_cols // HEAD_DIM
    pool_pages = kv_cache.shape[1]
    page_len = kv_cache.shape[2]
    data_devices = lax.axis_size("dp")
    requests = local_rows * data_devices
    score_scale = HEAD_DIM ** (-0.5)
    normed = rms_norm(hidden, attn_gain)
    projected = jnp.dot(
        normed, w_qkv.reshape(w_qkv.shape[0], 3 * head_cols), preferred_element_type=jnp.float32
    )
    projected = lax.optimization_barrier(projected.astype(jnp.bfloat16)).reshape(
        local_rows, 3, head_cols
    )
    appended = jnp.stack([projected[:, 1], projected[:, 2]])
    full_w_out = butterfly_gather(w_out, "mp")
    every_query = exchange_gather(projected[:, 0], "dp")
    own_queries = projected[:, 0].reshape(local_rows, local_heads, HEAD_DIM).astype(jnp.float32)
    own_keys = projected[:, 1].reshape(local_rows, local_heads, HEAD_DIM).astype(jnp.float32)
    own_values = projected[:, 2].reshape(local_rows, local_heads, HEAD_DIM).astype(jnp.float32)
    self_scores = jnp.sum(own_queries * own_keys, axis=-1) * score_scale
    home_row = lax.axis_index("dp") * local_rows
    request_ids = jnp.arange(requests, dtype=jnp.int32)
    offsets = jnp.arange(page_len, dtype=jnp.int32)

    owners = page_request
    clamped = jnp.maximum(owners, 0)
    chosen_queries = every_query[clamped]
    head_of_col = jnp.arange(head_cols, dtype=jnp.int32) // HEAD_DIM
    head_mask = head_of_col[:, None] == jnp.arange(local_heads, dtype=jnp.int32)[None, :]
    query_blocks = jnp.where(head_mask[None], chosen_queries[:, :, None], jnp.zeros((), jnp.bfloat16))
    key_rows = kv_cache[0]
    value_rows = kv_cache[1]
    scores = (
        jnp.einsum("ptc,pch->pth", key_rows, query_blocks, preferred_element_type=jnp.float32)
        * score_scale
    )
    position = page_index[:, None] * page_len + offsets[None, :]
    usable = (owners[:, None] >= 0) & (position < lengths[clamped][:, None])
    page_max = jnp.max(jnp.where(usable[:, :, None], scores, NEGATIVE), axis=1)
    raw = jnp.where(usable[:, :, None], jnp.exp(scores - page_max[:, None, :]), 0.0)
    page_total = jnp.sum(raw, axis=1)
    head_sums = jnp.einsum(
        "pth,ptc->phc", raw.astype(jnp.bfloat16), value_rows, preferred_element_type=jnp.float32
    )
    page_sum = jnp.sum(jnp.where(head_mask.T[None], head_sums, 0.0), axis=1)

    member = owners[:, None] == request_ids[None, :]
    seg_max = jnp.max(jnp.where(member[:, :, None], page_max[:, None, :], NEGATIVE), axis=0)
    self_full = lax.dynamic_update_slice(
        jnp.full((requests, local_heads), NEGATIVE, jnp.float32), self_scores, (home_row, 0)
    )
    local_max = jnp.maximum(seg_max, self_full)
    factors = jnp.where(owners[:, None] >= 0, jnp.exp(page_max - local_max[clamped]), 0.0)
    payload = jnp.concatenate(
        [page_sum * jnp.repeat(factors, HEAD_DIM, axis=1), page_total * factors],
        axis=1,
    )
    onehot = member.astype(jnp.float32)
    local_sums = jnp.einsum("pr,pc->rc", onehot, payload, precision=lax.Precision.HIGHEST)
    home_max = lax.dynamic_slice_in_dim(local_max, home_row, local_rows, 0)
    self_weight = jnp.exp(self_scores - home_max)
    self_payload = jnp.concatenate(
        [(self_weight[:, :, None] * own_values).reshape(local_rows, head_cols), self_weight],
        axis=1,
    )
    local_sums = local_sums + lax.dynamic_update_slice(
        jnp.zeros_like(local_sums), self_payload, (home_row, 0)
    )

    lanes = 128
    stats = jnp.concatenate([local_sums[:, head_cols:], local_max], axis=1)
    stats = stats.reshape(data_devices, local_rows * 2 * local_heads)
    stats_rows = -(-stats.shape[1] // lanes)
    stats = jnp.pad(stats, ((0, 0), (0, stats_rows * lanes - stats.shape[1])))
    weighted_rows = local_rows * head_cols // lanes
    packed = jnp.concatenate(
        [
            local_sums[:, :head_cols].reshape(data_devices, weighted_rows, lanes),
            stats.reshape(data_devices, stats_rows, lanes),
        ],
        axis=1,
    )
    received = lax.all_to_all(packed, "dp", 0, 0, tiled=True)
    source_weighted = received[:, :weighted_rows].reshape(data_devices, local_rows, head_cols)
    source_stats = received[:, weighted_rows:].reshape(data_devices, stats_rows * lanes)
    source_stats = source_stats[:, : local_rows * 2 * local_heads].reshape(
        data_devices, local_rows, 2 * local_heads
    )
    source_totals = source_stats[:, :, :local_heads]
    source_max = source_stats[:, :, local_heads:]
    global_max = jnp.max(source_max, axis=0)
    shrink = jnp.exp(source_max - global_max[None])
    mine = jnp.concatenate(
        [
            jnp.sum(source_weighted * jnp.repeat(shrink, HEAD_DIM, axis=2), axis=0),
            jnp.sum(source_totals * shrink, axis=0),
        ],
        axis=1,
    )
    own_weighted = mine[:, :head_cols].reshape(local_rows, local_heads, HEAD_DIM)
    own_totals = mine[:, head_cols:]
    context = (
        (own_weighted / own_totals[:, :, None]).reshape(local_rows, head_cols).astype(jnp.bfloat16)
    )
    model_devices = lax.axis_size("mp")
    every_context = exchange_gather(context, "mp")
    every_context = every_context.reshape(model_devices, local_rows, head_cols)
    every_context = every_context.transpose(1, 0, 2).reshape(local_rows, model_devices * head_cols)
    attended = jnp.dot(every_context, full_w_out, preferred_element_type=jnp.float32)
    residual = lax.optimization_barrier(
        (hidden.astype(jnp.float32) + attended).astype(jnp.bfloat16)
    )
    normed_mlp = rms_norm(residual, mlp_gain)
    hidden_cols = w_gate_up.shape[2]
    gate_up = jnp.dot(
        normed_mlp,
        w_gate_up.reshape(w_gate_up.shape[0], 2 * hidden_cols),
        preferred_element_type=jnp.float32,
    ).reshape(local_rows, 2, hidden_cols)
    activated = (jax.nn.silu(gate_up[:, 0]) * gate_up[:, 1]).astype(jnp.bfloat16)
    lowered = butterfly_sum(jnp.dot(activated, w_down, preferred_element_type=jnp.float32), "mp")
    hidden_out = (residual.astype(jnp.float32) + lowered).astype(jnp.bfloat16)
    return (appended, hidden_out)


def solution(mesh):
    return jax.shard_map(
        body,
        mesh=mesh,
        in_specs=(
            P("dp", None),
            P(),
            P(None, None, "mp"),
            P("mp", None),
            P(),
            P(None, None, "mp"),
            P("mp", None),
            P(None, "dp", None, "mp"),
            P(),
            P("dp"),
            P("dp"),
        ),
        out_specs=(P(None, "dp", "mp"), P("dp", None)),
        check_vma=False,
    )
```

```python
import jax
import jax.numpy as jnp
from jax import lax
from jax.sharding import PartitionSpec as P

HEAD_DIM = 64


EPSILON = 1e-05
NEGATIVE = -1e30


def rms_norm(values, gain):
    widened = values.astype(jnp.float32)
    mean_square = jnp.mean(widened * widened, axis=-1, keepdims=True)
    return (widened * lax.rsqrt(mean_square + EPSILON) * gain).astype(jnp.bfloat16)


def butterfly_sum(value, axis):
    size = lax.axis_size(axis)
    if size & (size - 1):
        return lax.psum(value, axis)
    distance = 1
    while distance < size:
        pairs = [(j, j ^ distance) for j in range(size)]
        value = value + lax.ppermute(value, axis, pairs)
        distance *= 2
    return value


def exchange_gather(value, axis):
    size = lax.axis_size(axis)
    spread = jnp.broadcast_to(value[None], (size,) + value.shape)
    gathered = lax.all_to_all(spread, axis, 0, 0, tiled=True)
    return gathered.reshape((size * value.shape[0],) + value.shape[1:])


def butterfly_gather(value, axis):
    size = lax.axis_size(axis)
    if size & (size - 1):
        return lax.all_gather(value, axis, axis=0, tiled=True)
    me = lax.axis_index(axis)
    distance = 1
    while distance < size:
        pairs = [(j, j ^ distance) for j in range(size)]
        other = lax.ppermute(value, axis, pairs)
        low = (me & distance) == 0
        value = jnp.where(
            low, jnp.concatenate([value, other], 0), jnp.concatenate([other, value], 0)
        )
        distance *= 2
    return value


def body(
    hidden,
    attn_gain,
    w_qkv,
    w_out,
    mlp_gain,
    w_gate_up,
    w_down,
    kv_cache,
    lengths,
    page_request,
    page_index,
):
    local_rows = hidden.shape[0]
    head_cols = w_qkv.shape[2]
    local_heads = head_cols // HEAD_DIM
    pool_pages = kv_cache.shape[1]
    page_len = kv_cache.shape[2]
    data_devices = lax.axis_size("dp")
    requests = local_rows * data_devices
    score_scale = HEAD_DIM ** (-0.5)
    normed = rms_norm(hidden, attn_gain)
    projected = jnp.einsum("rd,dkc->rkc", normed, w_qkv, preferred_element_type=jnp.float32)
    projected = lax.optimization_barrier(projected.astype(jnp.bfloat16))
    appended = jnp.stack([projected[:, 1], projected[:, 2]])
    every_query = exchange_gather(projected[:, 0], "dp")
    own_queries = projected[:, 0].reshape(local_rows, local_heads, HEAD_DIM).astype(jnp.float32)
    own_keys = projected[:, 1].reshape(local_rows, local_heads, HEAD_DIM).astype(jnp.float32)
    own_values = projected[:, 2].reshape(local_rows, local_heads, HEAD_DIM).astype(jnp.float32)
    self_scores = jnp.sum(own_queries * own_keys, axis=-1) * score_scale
    home_row = lax.axis_index("dp") * local_rows
    request_ids = jnp.arange(requests, dtype=jnp.int32)
    offsets = jnp.arange(page_len, dtype=jnp.int32)

    owners = page_request
    clamped = jnp.maximum(owners, 0)
    chosen_queries = every_query[clamped]
    head_of_col = jnp.arange(head_cols, dtype=jnp.int32) // HEAD_DIM
    head_mask = head_of_col[:, None] == jnp.arange(local_heads, dtype=jnp.int32)[None, :]
    query_blocks = jnp.where(head_mask[None], chosen_queries[:, :, None], jnp.zeros((), jnp.bfloat16))
    key_rows = kv_cache[0]
    value_rows = kv_cache[1]
    scores = (
        jnp.einsum("ptc,pch->pth", key_rows, query_blocks, preferred_element_type=jnp.float32)
        * score_scale
    )
    position = page_index[:, None] * page_len + offsets[None, :]
    usable = (owners[:, None] >= 0) & (position < lengths[clamped][:, None])
    page_max = jnp.max(jnp.where(usable[:, :, None], scores, NEGATIVE), axis=1)
    raw = jnp.where(usable[:, :, None], jnp.exp(scores - page_max[:, None, :]), 0.0)
    page_total = jnp.sum(raw, axis=1)
    head_sums = jnp.einsum(
        "pth,ptc->phc", raw.astype(jnp.bfloat16), value_rows, preferred_element_type=jnp.float32
    )
    page_sum = jnp.sum(jnp.where(head_mask.T[None], head_sums, 0.0), axis=1)

    member = owners[:, None] == request_ids[None, :]
    seg_max = jnp.max(jnp.where(member[:, :, None], page_max[:, None, :], NEGATIVE), axis=0)
    self_full = lax.dynamic_update_slice(
        jnp.full((requests, local_heads), NEGATIVE, jnp.float32), self_scores, (home_row, 0)
    )
    local_max = jnp.maximum(seg_max, self_full)
    factors = jnp.where(owners[:, None] >= 0, jnp.exp(page_max - local_max[clamped]), 0.0)
    payload = jnp.concatenate(
        [page_sum * jnp.repeat(factors, HEAD_DIM, axis=1), page_total * factors],
        axis=1,
    )
    onehot = member.astype(jnp.float32)
    local_sums = jnp.einsum("pr,pc->rc", onehot, payload, precision=lax.Precision.HIGHEST)
    home_max = lax.dynamic_slice_in_dim(local_max, home_row, local_rows, 0)
    self_weight = jnp.exp(self_scores - home_max)
    self_payload = jnp.concatenate(
        [(self_weight[:, :, None] * own_values).reshape(local_rows, head_cols), self_weight],
        axis=1,
    )
    local_sums = local_sums + lax.dynamic_update_slice(
        jnp.zeros_like(local_sums), self_payload, (home_row, 0)
    )

    lanes = 128
    stats = jnp.concatenate([local_sums[:, head_cols:], local_max], axis=1)
    stats = stats.reshape(data_devices, local_rows * 2 * local_heads)
    stats_rows = -(-stats.shape[1] // lanes)
    stats = jnp.pad(stats, ((0, 0), (0, stats_rows * lanes - stats.shape[1])))
    weighted_rows = local_rows * head_cols // lanes
    packed = jnp.concatenate(
        [
            local_sums[:, :head_cols].reshape(data_devices, weighted_rows, lanes),
            stats.reshape(data_devices, stats_rows, lanes),
        ],
        axis=1,
    )
    received = lax.all_to_all(packed, "dp", 0, 0, tiled=True)
    source_weighted = received[:, :weighted_rows].reshape(data_devices, local_rows, head_cols)
    source_stats = received[:, weighted_rows:].reshape(data_devices, stats_rows * lanes)
    source_stats = source_stats[:, : local_rows * 2 * local_heads].reshape(
        data_devices, local_rows, 2 * local_heads
    )
    source_totals = source_stats[:, :, :local_heads]
    source_max = source_stats[:, :, local_heads:]
    global_max = jnp.max(source_max, axis=0)
    shrink = jnp.exp(source_max - global_max[None])
    mine = jnp.concatenate(
        [
            jnp.sum(source_weighted * jnp.repeat(shrink, HEAD_DIM, axis=2), axis=0),
            jnp.sum(source_totals * shrink, axis=0),
        ],
        axis=1,
    )
    own_weighted = mine[:, :head_cols].reshape(local_rows, local_heads, HEAD_DIM)
    own_totals = mine[:, head_cols:]
    context = (
        (own_weighted / own_totals[:, :, None]).reshape(local_rows, head_cols).astype(jnp.bfloat16)
    )
    attended = butterfly_sum(jnp.dot(context, w_out, preferred_element_type=jnp.float32), "mp")
    residual = lax.optimization_barrier(
        (hidden.astype(jnp.float32) + attended).astype(jnp.bfloat16)
    )
    normed_mlp = rms_norm(residual, mlp_gain)
    hidden_cols = w_gate_up.shape[2]
    gate_up = jnp.einsum("rd,dkc->rkc", normed_mlp, w_gate_up, preferred_element_type=jnp.float32)
    activated = (jax.nn.silu(gate_up[:, 0]) * gate_up[:, 1]).astype(jnp.bfloat16)
    lowered = butterfly_sum(jnp.dot(activated, w_down, preferred_element_type=jnp.float32), "mp")
    hidden_out = (residual.astype(jnp.float32) + lowered).astype(jnp.bfloat16)
    return (appended, hidden_out)


def solution(mesh):
    return jax.shard_map(
        body,
        mesh=mesh,
        in_specs=(
            P("dp", None),
            P(),
            P(None, None, "mp"),
            P("mp", None),
            P(),
            P(None, None, "mp"),
            P("mp", None),
            P(None, "dp", None, "mp"),
            P(),
            P("dp"),
            P("dp"),
        ),
        out_specs=(P(None, "dp", "mp"), P("dp", None)),
        check_vma=False,
    )
```

```python
import jax
import jax.numpy as jnp
from jax import lax
from jax.sharding import PartitionSpec as P

HEAD_DIM = 64


EPSILON = 1e-05
NEGATIVE = -1e30


def rms_norm(values, gain):
    widened = values.astype(jnp.float32)
    mean_square = jnp.mean(widened * widened, axis=-1, keepdims=True)
    return (widened * lax.rsqrt(mean_square + EPSILON) * gain).astype(jnp.bfloat16)


def butterfly_sum(value, axis):
    size = lax.axis_size(axis)
    if size & (size - 1):
        return lax.psum(value, axis)
    distance = 1
    while distance < size:
        pairs = [(j, j ^ distance) for j in range(size)]
        value = value + lax.ppermute(value, axis, pairs)
        distance *= 2
    return value


def exchange_gather(value, axis):
    size = lax.axis_size(axis)
    spread = jnp.broadcast_to(value[None], (size,) + value.shape)
    gathered = lax.all_to_all(spread, axis, 0, 0, tiled=True)
    return gathered.reshape((size * value.shape[0],) + value.shape[1:])


def butterfly_gather(value, axis):
    size = lax.axis_size(axis)
    if size & (size - 1):
        return lax.all_gather(value, axis, axis=0, tiled=True)
    me = lax.axis_index(axis)
    distance = 1
    while distance < size:
        pairs = [(j, j ^ distance) for j in range(size)]
        other = lax.ppermute(value, axis, pairs)
        low = (me & distance) == 0
        value = jnp.where(
            low, jnp.concatenate([value, other], 0), jnp.concatenate([other, value], 0)
        )
        distance *= 2
    return value


def body(
    hidden,
    attn_gain,
    w_qkv,
    w_out,
    mlp_gain,
    w_gate_up,
    w_down,
    kv_cache,
    lengths,
    page_request,
    page_index,
):
    local_rows = hidden.shape[0]
    head_cols = w_qkv.shape[2]
    local_heads = head_cols // HEAD_DIM
    pool_pages = kv_cache.shape[1]
    page_len = kv_cache.shape[2]
    data_devices = lax.axis_size("dp")
    requests = local_rows * data_devices
    score_scale = HEAD_DIM ** (-0.5)
    normed = rms_norm(hidden, attn_gain)
    projected = jnp.einsum("rd,dkc->rkc", normed, w_qkv, preferred_element_type=jnp.float32)
    projected = lax.optimization_barrier(projected.astype(jnp.bfloat16))
    appended = jnp.stack([projected[:, 1], projected[:, 2]])
    every_query = exchange_gather(projected[:, 0], "dp")
    own_queries = projected[:, 0].reshape(local_rows, local_heads, HEAD_DIM).astype(jnp.float32)
    own_keys = projected[:, 1].reshape(local_rows, local_heads, HEAD_DIM).astype(jnp.float32)
    own_values = projected[:, 2].reshape(local_rows, local_heads, HEAD_DIM).astype(jnp.float32)
    self_scores = jnp.sum(own_queries * own_keys, axis=-1) * score_scale
    home_row = lax.axis_index("dp") * local_rows
    request_ids = jnp.arange(requests, dtype=jnp.int32)
    offsets = jnp.arange(page_len, dtype=jnp.int32)

    owners = page_request
    clamped = jnp.maximum(owners, 0)
    chosen_queries = every_query[clamped]
    head_of_col = jnp.arange(head_cols, dtype=jnp.int32) // HEAD_DIM
    head_mask = head_of_col[:, None] == jnp.arange(local_heads, dtype=jnp.int32)[None, :]
    query_blocks = jnp.where(head_mask.T[None], chosen_queries[:, None, :], jnp.zeros((), jnp.bfloat16))
    key_rows = kv_cache[0]
    value_rows = kv_cache[1]
    scores = (
        jnp.einsum("phc,ptc->pht", query_blocks, key_rows, preferred_element_type=jnp.float32)
        * score_scale
    )
    position = page_index[:, None] * page_len + offsets[None, :]
    usable = (owners[:, None] >= 0) & (position < lengths[clamped][:, None])
    page_max = jnp.max(jnp.where(usable[:, None, :], scores, NEGATIVE), axis=2)
    raw = jnp.where(usable[:, None, :], jnp.exp(scores - page_max[:, :, None]), 0.0)
    page_total = jnp.sum(raw, axis=2)
    head_sums = jnp.einsum(
        "pht,ptc->phc", raw.astype(jnp.bfloat16), value_rows, preferred_element_type=jnp.float32
    )
    page_sum = jnp.sum(jnp.where(head_mask.T[None], head_sums, 0.0), axis=1)

    member = owners[:, None] == request_ids[None, :]
    seg_max = jnp.max(jnp.where(member[:, :, None], page_max[:, None, :], NEGATIVE), axis=0)
    self_full = lax.dynamic_update_slice(
        jnp.full((requests, local_heads), NEGATIVE, jnp.float32), self_scores, (home_row, 0)
    )
    local_max = jnp.maximum(seg_max, self_full)
    factors = jnp.where(owners[:, None] >= 0, jnp.exp(page_max - local_max[clamped]), 0.0)
    payload = jnp.concatenate(
        [page_sum * jnp.repeat(factors, HEAD_DIM, axis=1), page_total * factors],
        axis=1,
    )
    onehot = member.astype(jnp.float32)
    local_sums = jnp.einsum("pr,pc->rc", onehot, payload, precision=lax.Precision.HIGHEST)
    home_max = lax.dynamic_slice_in_dim(local_max, home_row, local_rows, 0)
    self_weight = jnp.exp(self_scores - home_max)
    self_payload = jnp.concatenate(
        [(self_weight[:, :, None] * own_values).reshape(local_rows, head_cols), self_weight],
        axis=1,
    )
    local_sums = local_sums + lax.dynamic_update_slice(
        jnp.zeros_like(local_sums), self_payload, (home_row, 0)
    )

    lanes = 128
    stats = jnp.concatenate([local_sums[:, head_cols:], local_max], axis=1)
    stats = stats.reshape(data_devices, local_rows * 2 * local_heads)
    stats_rows = -(-stats.shape[1] // lanes)
    stats = jnp.pad(stats, ((0, 0), (0, stats_rows * lanes - stats.shape[1])))
    weighted_rows = local_rows * head_cols // lanes
    packed = jnp.concatenate(
        [
            local_sums[:, :head_cols].reshape(data_devices, weighted_rows, lanes),
            stats.reshape(data_devices, stats_rows, lanes),
        ],
        axis=1,
    )
    received = lax.all_to_all(packed, "dp", 0, 0, tiled=True)
    source_weighted = received[:, :weighted_rows].reshape(data_devices, local_rows, head_cols)
    source_stats = received[:, weighted_rows:].reshape(data_devices, stats_rows * lanes)
    source_stats = source_stats[:, : local_rows * 2 * local_heads].reshape(
        data_devices, local_rows, 2 * local_heads
    )
    source_totals = source_stats[:, :, :local_heads]
    source_max = source_stats[:, :, local_heads:]
    global_max = jnp.max(source_max, axis=0)
    shrink = jnp.exp(source_max - global_max[None])
    mine = jnp.concatenate(
        [
            jnp.sum(source_weighted * jnp.repeat(shrink, HEAD_DIM, axis=2), axis=0),
            jnp.sum(source_totals * shrink, axis=0),
        ],
        axis=1,
    )
    own_weighted = mine[:, :head_cols].reshape(local_rows, local_heads, HEAD_DIM)
    own_totals = mine[:, head_cols:]
    context = (
        (own_weighted / own_totals[:, :, None]).reshape(local_rows, head_cols).astype(jnp.bfloat16)
    )
    attended = butterfly_sum(jnp.dot(context, w_out, preferred_element_type=jnp.float32), "mp")
    residual = lax.optimization_barrier(
        (hidden.astype(jnp.float32) + attended).astype(jnp.bfloat16)
    )
    normed_mlp = rms_norm(residual, mlp_gain)
    hidden_cols = w_gate_up.shape[2]
    gate_up = jnp.einsum("rd,dkc->rkc", normed_mlp, w_gate_up, preferred_element_type=jnp.float32)
    activated = (jax.nn.silu(gate_up[:, 0]) * gate_up[:, 1]).astype(jnp.bfloat16)
    lowered = butterfly_sum(jnp.dot(activated, w_down, preferred_element_type=jnp.float32), "mp")
    hidden_out = (residual.astype(jnp.float32) + lowered).astype(jnp.bfloat16)
    return (appended, hidden_out)


def solution(mesh):
    return jax.shard_map(
        body,
        mesh=mesh,
        in_specs=(
            P("dp", None),
            P(),
            P(None, None, "mp"),
            P("mp", None),
            P(),
            P(None, None, "mp"),
            P("mp", None),
            P(None, "dp", None, "mp"),
            P(),
            P("dp"),
            P("dp"),
        ),
        out_specs=(P(None, "dp", "mp"), P("dp", None)),
        check_vma=False,
    )
```

```python
import jax
import jax.numpy as jnp
from jax import lax
from jax.sharding import PartitionSpec as P

HEAD_DIM = 64


EPSILON = 1e-05
NEGATIVE = -1e30


def rms_norm(values, gain):
    widened = values.astype(jnp.float32)
    mean_square = jnp.mean(widened * widened, axis=-1, keepdims=True)
    return (widened * lax.rsqrt(mean_square + EPSILON) * gain).astype(jnp.bfloat16)


def butterfly_sum(value, axis):
    size = lax.axis_size(axis)
    if size & (size - 1):
        return lax.psum(value, axis)
    distance = 1
    while distance < size:
        pairs = [(j, j ^ distance) for j in range(size)]
        if size == 8 and distance == 4:
            pairs = [(0, 6), (6, 0), (1, 7), (7, 1), (2, 4), (4, 2), (3, 5), (5, 3)]
        value = value + lax.ppermute(value, axis, pairs)
        distance *= 2
    return value


def exchange_gather(value, axis):
    size = lax.axis_size(axis)
    spread = jnp.broadcast_to(value[None], (size,) + value.shape)
    gathered = lax.all_to_all(spread, axis, 0, 0, tiled=True)
    return gathered.reshape((size * value.shape[0],) + value.shape[1:])


def butterfly_gather(value, axis):
    size = lax.axis_size(axis)
    if size & (size - 1):
        return lax.all_gather(value, axis, axis=0, tiled=True)
    me = lax.axis_index(axis)
    distance = 1
    while distance < size:
        pairs = [(j, j ^ distance) for j in range(size)]
        other = lax.ppermute(value, axis, pairs)
        low = (me & distance) == 0
        value = jnp.where(
            low, jnp.concatenate([value, other], 0), jnp.concatenate([other, value], 0)
        )
        distance *= 2
    return value


def body(
    hidden,
    attn_gain,
    w_qkv,
    w_out,
    mlp_gain,
    w_gate_up,
    w_down,
    kv_cache,
    lengths,
    page_request,
    page_index,
):
    local_rows = hidden.shape[0]
    head_cols = w_qkv.shape[2]
    local_heads = head_cols // HEAD_DIM
    pool_pages = kv_cache.shape[1]
    page_len = kv_cache.shape[2]
    data_devices = lax.axis_size("dp")
    requests = local_rows * data_devices
    score_scale = HEAD_DIM ** (-0.5)
    normed = rms_norm(hidden, attn_gain)
    projected = jnp.einsum("rd,dkc->rkc", normed, w_qkv, preferred_element_type=jnp.float32)
    projected = lax.optimization_barrier(projected.astype(jnp.bfloat16))
    appended = jnp.stack([projected[:, 1], projected[:, 2]])
    every_query = exchange_gather(projected[:, 0], "dp")
    own_queries = projected[:, 0].reshape(local_rows, local_heads, HEAD_DIM).astype(jnp.float32)
    own_keys = projected[:, 1].reshape(local_rows, local_heads, HEAD_DIM).astype(jnp.float32)
    own_values = projected[:, 2].reshape(local_rows, local_heads, HEAD_DIM).astype(jnp.float32)
    self_scores = jnp.sum(own_queries * own_keys, axis=-1) * score_scale
    home_row = lax.axis_index("dp") * local_rows
    request_ids = jnp.arange(requests, dtype=jnp.int32)
    offsets = jnp.arange(page_len, dtype=jnp.int32)

    owners = page_request
    clamped = jnp.maximum(owners, 0)
    chosen_queries = every_query[clamped]
    head_of_col = jnp.arange(head_cols, dtype=jnp.int32) // HEAD_DIM
    head_mask = head_of_col[:, None] == jnp.arange(local_heads, dtype=jnp.int32)[None, :]
    query_blocks = jnp.where(head_mask[None], chosen_queries[:, :, None], jnp.zeros((), jnp.bfloat16))
    key_rows = kv_cache[0]
    value_rows = kv_cache[1]
    scores = (
        jnp.einsum("ptc,pch->pth", key_rows, query_blocks, preferred_element_type=jnp.float32)
        * score_scale
    )
    position = page_index[:, None] * page_len + offsets[None, :]
    usable = (owners[:, None] >= 0) & (position < lengths[clamped][:, None])
    page_max = jnp.max(jnp.where(usable[:, :, None], scores, NEGATIVE), axis=1)
    raw = jnp.where(usable[:, :, None], jnp.exp(scores - page_max[:, None, :]), 0.0)
    page_total = jnp.sum(raw, axis=1)
    head_sums = jnp.einsum(
        "pth,ptc->phc", raw.astype(jnp.bfloat16), value_rows, preferred_element_type=jnp.float32
    )
    page_sum = jnp.sum(jnp.where(head_mask.T[None], head_sums, 0.0), axis=1)

    member = owners[:, None] == request_ids[None, :]
    seg_max = jnp.max(jnp.where(member[:, :, None], page_max[:, None, :], NEGATIVE), axis=0)
    self_full = lax.dynamic_update_slice(
        jnp.full((requests, local_heads), NEGATIVE, jnp.float32), self_scores, (home_row, 0)
    )
    local_max = jnp.maximum(seg_max, self_full)
    factors = jnp.where(owners[:, None] >= 0, jnp.exp(page_max - local_max[clamped]), 0.0)
    payload = jnp.concatenate(
        [page_sum * jnp.repeat(factors, HEAD_DIM, axis=1), page_total * factors],
        axis=1,
    )
    onehot = member.astype(jnp.float32)
    local_sums = jnp.einsum("pr,pc->rc", onehot, payload, precision=lax.Precision.HIGHEST)
    home_max = lax.dynamic_slice_in_dim(local_max, home_row, local_rows, 0)
    self_weight = jnp.exp(self_scores - home_max)
    self_payload = jnp.concatenate(
        [(self_weight[:, :, None] * own_values).reshape(local_rows, head_cols), self_weight],
        axis=1,
    )
    local_sums = local_sums + lax.dynamic_update_slice(
        jnp.zeros_like(local_sums), self_payload, (home_row, 0)
    )

    lanes = 128
    stats = jnp.concatenate([local_sums[:, head_cols:], local_max], axis=1)
    stats = stats.reshape(data_devices, local_rows * 2 * local_heads)
    stats_rows = -(-stats.shape[1] // lanes)
    stats = jnp.pad(stats, ((0, 0), (0, stats_rows * lanes - stats.shape[1])))
    weighted_rows = local_rows * head_cols // lanes
    packed = jnp.concatenate(
        [
            local_sums[:, :head_cols].reshape(data_devices, weighted_rows, lanes),
            stats.reshape(data_devices, stats_rows, lanes),
        ],
        axis=1,
    )
    received = lax.all_to_all(packed, "dp", 0, 0, tiled=True)
    source_weighted = received[:, :weighted_rows].reshape(data_devices, local_rows, head_cols)
    source_stats = received[:, weighted_rows:].reshape(data_devices, stats_rows * lanes)
    source_stats = source_stats[:, : local_rows * 2 * local_heads].reshape(
        data_devices, local_rows, 2 * local_heads
    )
    source_totals = source_stats[:, :, :local_heads]
    source_max = source_stats[:, :, local_heads:]
    global_max = jnp.max(source_max, axis=0)
    shrink = jnp.exp(source_max - global_max[None])
    mine = jnp.concatenate(
        [
            jnp.sum(source_weighted * jnp.repeat(shrink, HEAD_DIM, axis=2), axis=0),
            jnp.sum(source_totals * shrink, axis=0),
        ],
        axis=1,
    )
    own_weighted = mine[:, :head_cols].reshape(local_rows, local_heads, HEAD_DIM)
    own_totals = mine[:, head_cols:]
    context = (
        (own_weighted / own_totals[:, :, None]).reshape(local_rows, head_cols).astype(jnp.bfloat16)
    )
    attended = butterfly_sum(jnp.dot(context, w_out, preferred_element_type=jnp.float32), "mp")
    residual = lax.optimization_barrier(
        (hidden.astype(jnp.float32) + attended).astype(jnp.bfloat16)
    )
    normed_mlp = rms_norm(residual, mlp_gain)
    hidden_cols = w_gate_up.shape[2]
    gate_up = jnp.einsum("rd,dkc->rkc", normed_mlp, w_gate_up, preferred_element_type=jnp.float32)
    activated = (jax.nn.silu(gate_up[:, 0]) * gate_up[:, 1]).astype(jnp.bfloat16)
    lowered = butterfly_sum(jnp.dot(activated, w_down, preferred_element_type=jnp.float32), "mp")
    hidden_out = (residual.astype(jnp.float32) + lowered).astype(jnp.bfloat16)
    return (appended, hidden_out)


def solution(mesh):
    return jax.shard_map(
        body,
        mesh=mesh,
        in_specs=(
            P("dp", None),
            P(),
            P(None, None, "mp"),
            P("mp", None),
            P(),
            P(None, None, "mp"),
            P("mp", None),
            P(None, "dp", None, "mp"),
            P(),
            P("dp"),
            P("dp"),
        ),
        out_specs=(P(None, "dp", "mp"), P("dp", None)),
        check_vma=False,
    )
```

```python
import jax
import jax.numpy as jnp
from jax import lax
from jax.sharding import PartitionSpec as P

HEAD_DIM = 64


EPSILON = 1e-05
NEGATIVE = -1e30


def rms_norm(values, gain):
    widened = values.astype(jnp.float32)
    mean_square = jnp.mean(widened * widened, axis=-1, keepdims=True)
    return (widened * lax.rsqrt(mean_square + EPSILON) * gain).astype(jnp.bfloat16)


def butterfly_sum(value, axis):
    size = lax.axis_size(axis)
    if size & (size - 1):
        return lax.psum(value, axis)
    distance = 1
    while distance < size:
        pairs = [(j, j ^ distance) for j in range(size)]
        if size == 8 and distance == 4:
            pairs = [(0, 6), (6, 0), (1, 7), (7, 1), (2, 4), (4, 2), (3, 5), (5, 3)]
        value = value + lax.ppermute(value, axis, pairs)
        distance *= 2
    return value


def exchange_gather(value, axis):
    size = lax.axis_size(axis)
    spread = jnp.broadcast_to(value[None], (size,) + value.shape)
    gathered = lax.all_to_all(spread, axis, 0, 0, tiled=True)
    return gathered.reshape((size * value.shape[0],) + value.shape[1:])


def butterfly_gather(value, axis):
    size = lax.axis_size(axis)
    if size & (size - 1):
        return lax.all_gather(value, axis, axis=0, tiled=True)
    me = lax.axis_index(axis)
    distance = 1
    while distance < size:
        pairs = [(j, j ^ distance) for j in range(size)]
        other = lax.ppermute(value, axis, pairs)
        low = (me & distance) == 0
        value = jnp.where(
            low, jnp.concatenate([value, other], 0), jnp.concatenate([other, value], 0)
        )
        distance *= 2
    return value


def body(
    hidden,
    attn_gain,
    w_qkv,
    w_out,
    mlp_gain,
    w_gate_up,
    w_down,
    kv_cache,
    lengths,
    page_request,
    page_index,
):
    local_rows = hidden.shape[0]
    head_cols = w_qkv.shape[2]
    local_heads = head_cols // HEAD_DIM
    pool_pages = kv_cache.shape[1]
    page_len = kv_cache.shape[2]
    data_devices = lax.axis_size("dp")
    requests = local_rows * data_devices
    score_scale = HEAD_DIM ** (-0.5)
    normed = rms_norm(hidden, attn_gain)
    query_part = jnp.einsum(
        "rd,dc->rc", normed, w_qkv[:, 0, :], preferred_element_type=jnp.float32
    ).astype(jnp.bfloat16)
    every_query = exchange_gather(query_part, "dp")
    key_value_part = jnp.einsum(
        "rd,dkc->rkc", normed, w_qkv[:, 1:, :], preferred_element_type=jnp.float32
    ).astype(jnp.bfloat16)
    projected = lax.optimization_barrier(
        jnp.concatenate([query_part[:, None, :], key_value_part], axis=1)
    )
    appended = jnp.stack([projected[:, 1], projected[:, 2]])
    own_queries = projected[:, 0].reshape(local_rows, local_heads, HEAD_DIM).astype(jnp.float32)
    own_keys = projected[:, 1].reshape(local_rows, local_heads, HEAD_DIM).astype(jnp.float32)
    own_values = projected[:, 2].reshape(local_rows, local_heads, HEAD_DIM).astype(jnp.float32)
    self_scores = jnp.sum(own_queries * own_keys, axis=-1) * score_scale
    home_row = lax.axis_index("dp") * local_rows
    request_ids = jnp.arange(requests, dtype=jnp.int32)
    offsets = jnp.arange(page_len, dtype=jnp.int32)

    owners = page_request
    clamped = jnp.maximum(owners, 0)
    chosen_queries = every_query[clamped]
    head_of_col = jnp.arange(head_cols, dtype=jnp.int32) // HEAD_DIM
    head_mask = head_of_col[:, None] == jnp.arange(local_heads, dtype=jnp.int32)[None, :]
    query_blocks = jnp.where(head_mask[None], chosen_queries[:, :, None], jnp.zeros((), jnp.bfloat16))
    key_rows = kv_cache[0]
    value_rows = kv_cache[1]
    scores = (
        jnp.einsum("ptc,pch->pth", key_rows, query_blocks, preferred_element_type=jnp.float32)
        * score_scale
    )
    position = page_index[:, None] * page_len + offsets[None, :]
    usable = (owners[:, None] >= 0) & (position < lengths[clamped][:, None])
    page_max = jnp.max(jnp.where(usable[:, :, None], scores, NEGATIVE), axis=1)
    raw = jnp.where(usable[:, :, None], jnp.exp(scores - page_max[:, None, :]), 0.0)
    page_total = jnp.sum(raw, axis=1)
    head_sums = jnp.einsum(
        "pth,ptc->phc", raw.astype(jnp.bfloat16), value_rows, preferred_element_type=jnp.float32
    )
    page_sum = jnp.sum(jnp.where(head_mask.T[None], head_sums, 0.0), axis=1)

    member = owners[:, None] == request_ids[None, :]
    seg_max = jnp.max(jnp.where(member[:, :, None], page_max[:, None, :], NEGATIVE), axis=0)
    self_full = lax.dynamic_update_slice(
        jnp.full((requests, local_heads), NEGATIVE, jnp.float32), self_scores, (home_row, 0)
    )
    local_max = jnp.maximum(seg_max, self_full)
    factors = jnp.where(owners[:, None] >= 0, jnp.exp(page_max - local_max[clamped]), 0.0)
    payload = jnp.concatenate(
        [page_sum * jnp.repeat(factors, HEAD_DIM, axis=1), page_total * factors],
        axis=1,
    )
    onehot = member.astype(jnp.float32)
    local_sums = jnp.einsum("pr,pc->rc", onehot, payload, precision=lax.Precision.HIGHEST)
    home_max = lax.dynamic_slice_in_dim(local_max, home_row, local_rows, 0)
    self_weight = jnp.exp(self_scores - home_max)
    self_payload = jnp.concatenate(
        [(self_weight[:, :, None] * own_values).reshape(local_rows, head_cols), self_weight],
        axis=1,
    )
    local_sums = local_sums + lax.dynamic_update_slice(
        jnp.zeros_like(local_sums), self_payload, (home_row, 0)
    )

    lanes = 128
    stats = jnp.concatenate([local_sums[:, head_cols:], local_max], axis=1)
    stats = stats.reshape(data_devices, local_rows * 2 * local_heads)
    stats_rows = -(-stats.shape[1] // lanes)
    stats = jnp.pad(stats, ((0, 0), (0, stats_rows * lanes - stats.shape[1])))
    weighted_rows = local_rows * head_cols // lanes
    packed = jnp.concatenate(
        [
            local_sums[:, :head_cols].reshape(data_devices, weighted_rows, lanes),
            stats.reshape(data_devices, stats_rows, lanes),
        ],
        axis=1,
    )
    received = lax.all_to_all(packed, "dp", 0, 0, tiled=True)
    source_weighted = received[:, :weighted_rows].reshape(data_devices, local_rows, head_cols)
    source_stats = received[:, weighted_rows:].reshape(data_devices, stats_rows * lanes)
    source_stats = source_stats[:, : local_rows * 2 * local_heads].reshape(
        data_devices, local_rows, 2 * local_heads
    )
    source_totals = source_stats[:, :, :local_heads]
    source_max = source_stats[:, :, local_heads:]
    global_max = jnp.max(source_max, axis=0)
    shrink = jnp.exp(source_max - global_max[None])
    mine = jnp.concatenate(
        [
            jnp.sum(source_weighted * jnp.repeat(shrink, HEAD_DIM, axis=2), axis=0),
            jnp.sum(source_totals * shrink, axis=0),
        ],
        axis=1,
    )
    own_weighted = mine[:, :head_cols].reshape(local_rows, local_heads, HEAD_DIM)
    own_totals = mine[:, head_cols:]
    context = (
        (own_weighted / own_totals[:, :, None]).reshape(local_rows, head_cols).astype(jnp.bfloat16)
    )
    attended = butterfly_sum(jnp.dot(context, w_out, preferred_element_type=jnp.float32), "mp")
    residual = lax.optimization_barrier(
        (hidden.astype(jnp.float32) + attended).astype(jnp.bfloat16)
    )
    normed_mlp = rms_norm(residual, mlp_gain)
    hidden_cols = w_gate_up.shape[2]
    gate_up = jnp.einsum("rd,dkc->rkc", normed_mlp, w_gate_up, preferred_element_type=jnp.float32)
    activated = (jax.nn.silu(gate_up[:, 0]) * gate_up[:, 1]).astype(jnp.bfloat16)
    lowered = butterfly_sum(jnp.dot(activated, w_down, preferred_element_type=jnp.float32), "mp")
    hidden_out = (residual.astype(jnp.float32) + lowered).astype(jnp.bfloat16)
    return (appended, hidden_out)


def solution(mesh):
    return jax.shard_map(
        body,
        mesh=mesh,
        in_specs=(
            P("dp", None),
            P(),
            P(None, None, "mp"),
            P("mp", None),
            P(),
            P(None, None, "mp"),
            P("mp", None),
            P(None, "dp", None, "mp"),
            P(),
            P("dp"),
            P("dp"),
        ),
        out_specs=(P(None, "dp", "mp"), P("dp", None)),
        check_vma=False,
    )
```

```python
import jax
import jax.numpy as jnp
from jax import lax
from jax.sharding import PartitionSpec as P

HEAD_DIM = 64


EPSILON = 1e-05
NEGATIVE = -1e30


def rms_norm(values, gain):
    widened = values.astype(jnp.float32)
    mean_square = jnp.mean(widened * widened, axis=-1, keepdims=True)
    return (widened * lax.rsqrt(mean_square + EPSILON) * gain).astype(jnp.bfloat16)


def butterfly_sum(value, axis):
    size = lax.axis_size(axis)
    if size & (size - 1):
        return lax.psum(value, axis)
    distance = 1
    while distance < size:
        pairs = [(j, j ^ distance) for j in range(size)]
        if size == 8 and distance == 4:
            pairs = [(0, 6), (6, 0), (1, 7), (7, 1), (2, 4), (4, 2), (3, 5), (5, 3)]
        value = value + lax.ppermute(value, axis, pairs)
        distance *= 2
    return value


def exchange_gather(value, axis):
    size = lax.axis_size(axis)
    spread = jnp.broadcast_to(value[None], (size,) + value.shape)
    gathered = lax.all_to_all(spread, axis, 0, 0, tiled=True)
    return gathered.reshape((size * value.shape[0],) + value.shape[1:])


def butterfly_gather(value, axis):
    size = lax.axis_size(axis)
    if size & (size - 1):
        return lax.all_gather(value, axis, axis=0, tiled=True)
    me = lax.axis_index(axis)
    distance = 1
    while distance < size:
        pairs = [(j, j ^ distance) for j in range(size)]
        other = lax.ppermute(value, axis, pairs)
        low = (me & distance) == 0
        value = jnp.where(
            low, jnp.concatenate([value, other], 0), jnp.concatenate([other, value], 0)
        )
        distance *= 2
    return value


def body(
    hidden,
    attn_gain,
    w_qkv,
    w_out,
    mlp_gain,
    w_gate_up,
    w_down,
    kv_cache,
    lengths,
    page_request,
    page_index,
):
    local_rows = hidden.shape[0]
    head_cols = w_qkv.shape[2]
    local_heads = head_cols // HEAD_DIM
    pool_pages = kv_cache.shape[1]
    page_len = kv_cache.shape[2]
    data_devices = lax.axis_size("dp")
    requests = local_rows * data_devices
    score_scale = HEAD_DIM ** (-0.5)
    normed = rms_norm(hidden, attn_gain)
    projected = jnp.einsum("rd,dkc->rkc", normed, w_qkv, preferred_element_type=jnp.float32)
    projected = lax.optimization_barrier(projected.astype(jnp.bfloat16))
    appended = jnp.stack([projected[:, 1], projected[:, 2]])
    every_query = exchange_gather(projected[:, 0], "dp")
    own_queries = projected[:, 0].reshape(local_rows, local_heads, HEAD_DIM).astype(jnp.float32)
    own_keys = projected[:, 1].reshape(local_rows, local_heads, HEAD_DIM).astype(jnp.float32)
    own_values = projected[:, 2].reshape(local_rows, local_heads, HEAD_DIM).astype(jnp.float32)
    self_scores = jnp.sum(own_queries * own_keys, axis=-1) * score_scale
    home_row = lax.axis_index("dp") * local_rows
    request_ids = jnp.arange(requests, dtype=jnp.int32)
    offsets = jnp.arange(page_len, dtype=jnp.int32)

    owners = page_request
    clamped = jnp.maximum(owners, 0)
    chosen_queries = every_query[clamped]
    head_of_col = jnp.arange(head_cols, dtype=jnp.int32) // HEAD_DIM
    head_mask = head_of_col[:, None] == jnp.arange(local_heads, dtype=jnp.int32)[None, :]
    query_blocks = jnp.where(head_mask[None], chosen_queries[:, :, None], jnp.zeros((), jnp.bfloat16))
    key_rows = kv_cache[0]
    value_rows = kv_cache[1]
    scores = (
        jnp.einsum("ptc,pch->pth", key_rows, query_blocks, preferred_element_type=jnp.float32)
        * score_scale
    )
    position = page_index[:, None] * page_len + offsets[None, :]
    usable = (owners[:, None] >= 0) & (position < lengths[clamped][:, None])
    page_max = jnp.max(jnp.where(usable[:, :, None], scores, NEGATIVE), axis=1)
    raw = jnp.where(usable[:, :, None], jnp.exp(scores - page_max[:, None, :]), 0.0)
    page_total = jnp.sum(raw, axis=1)
    head_sums = jnp.einsum(
        "pth,ptc->phc", raw.astype(jnp.bfloat16), value_rows, preferred_element_type=jnp.float32
    )
    page_sum = jnp.sum(jnp.where(head_mask.T[None], head_sums, 0.0), axis=1)

    member = owners[:, None] == request_ids[None, :]
    seg_max = jnp.max(jnp.where(member[:, :, None], page_max[:, None, :], NEGATIVE), axis=0)
    self_full = lax.dynamic_update_slice(
        jnp.full((requests, local_heads), NEGATIVE, jnp.float32), self_scores, (home_row, 0)
    )
    local_max = jnp.maximum(seg_max, self_full)
    factors = jnp.where(owners[:, None] >= 0, jnp.exp(page_max - local_max[clamped]), 0.0)
    payload = jnp.concatenate(
        [page_sum * jnp.repeat(factors, HEAD_DIM, axis=1), page_total * factors],
        axis=1,
    )
    onehot = member.astype(jnp.float32)
    payload_high = payload.astype(jnp.bfloat16)
    payload_low = (payload - payload_high.astype(jnp.float32)).astype(jnp.bfloat16)
    onehot_bf16 = onehot.astype(jnp.bfloat16)
    local_sums = jnp.einsum(
        "pr,pc->rc", onehot_bf16, payload_high, preferred_element_type=jnp.float32
    ) + jnp.einsum("pr,pc->rc", onehot_bf16, payload_low, preferred_element_type=jnp.float32)
    home_max = lax.dynamic_slice_in_dim(local_max, home_row, local_rows, 0)
    self_weight = jnp.exp(self_scores - home_max)
    self_payload = jnp.concatenate(
        [(self_weight[:, :, None] * own_values).reshape(local_rows, head_cols), self_weight],
        axis=1,
    )
    local_sums = local_sums + lax.dynamic_update_slice(
        jnp.zeros_like(local_sums), self_payload, (home_row, 0)
    )

    lanes = 128
    stats = jnp.concatenate([local_sums[:, head_cols:], local_max], axis=1)
    stats = stats.reshape(data_devices, local_rows * 2 * local_heads)
    stats_rows = -(-stats.shape[1] // lanes)
    stats = jnp.pad(stats, ((0, 0), (0, stats_rows * lanes - stats.shape[1])))
    weighted_rows = local_rows * head_cols // lanes
    packed = jnp.concatenate(
        [
            local_sums[:, :head_cols].reshape(data_devices, weighted_rows, lanes),
            stats.reshape(data_devices, stats_rows, lanes),
        ],
        axis=1,
    )
    received = lax.all_to_all(packed, "dp", 0, 0, tiled=True)
    source_weighted = received[:, :weighted_rows].reshape(data_devices, local_rows, head_cols)
    source_stats = received[:, weighted_rows:].reshape(data_devices, stats_rows * lanes)
    source_stats = source_stats[:, : local_rows * 2 * local_heads].reshape(
        data_devices, local_rows, 2 * local_heads
    )
    source_totals = source_stats[:, :, :local_heads]
    source_max = source_stats[:, :, local_heads:]
    global_max = jnp.max(source_max, axis=0)
    shrink = jnp.exp(source_max - global_max[None])
    mine = jnp.concatenate(
        [
            jnp.sum(source_weighted * jnp.repeat(shrink, HEAD_DIM, axis=2), axis=0),
            jnp.sum(source_totals * shrink, axis=0),
        ],
        axis=1,
    )
    own_weighted = mine[:, :head_cols].reshape(local_rows, local_heads, HEAD_DIM)
    own_totals = mine[:, head_cols:]
    context = (
        (own_weighted / own_totals[:, :, None]).reshape(local_rows, head_cols).astype(jnp.bfloat16)
    )
    attended = butterfly_sum(jnp.dot(context, w_out, preferred_element_type=jnp.float32), "mp")
    residual = lax.optimization_barrier(
        (hidden.astype(jnp.float32) + attended).astype(jnp.bfloat16)
    )
    normed_mlp = rms_norm(residual, mlp_gain)
    hidden_cols = w_gate_up.shape[2]
    gate_up = jnp.einsum("rd,dkc->rkc", normed_mlp, w_gate_up, preferred_element_type=jnp.float32)
    activated = (jax.nn.silu(gate_up[:, 0]) * gate_up[:, 1]).astype(jnp.bfloat16)
    lowered = butterfly_sum(jnp.dot(activated, w_down, preferred_element_type=jnp.float32), "mp")
    hidden_out = (residual.astype(jnp.float32) + lowered).astype(jnp.bfloat16)
    return (appended, hidden_out)


def solution(mesh):
    return jax.shard_map(
        body,
        mesh=mesh,
        in_specs=(
            P("dp", None),
            P(),
            P(None, None, "mp"),
            P("mp", None),
            P(),
            P(None, None, "mp"),
            P("mp", None),
            P(None, "dp", None, "mp"),
            P(),
            P("dp"),
            P("dp"),
        ),
        out_specs=(P(None, "dp", "mp"), P("dp", None)),
        check_vma=False,
    )
```
